32 devices in a mesh: grp: 2 (over y), mem: 4 (over z), lev: 2 (over x), half: 2 (over core).
Axes of the slice: x: 2, y: 2, z: 4, core: 2. Of those that a mesh axis runs over, the one named last changes fastest.
Arguments:
- anomalies: bfloat16 [512, 48, 4, 512], P('half', ('grp', 'mem'), 'lev'), parts along dimension 1, may hold values from -3.5 to 3.5
- control: bfloat16 [256, 48, 4, 256], P('half', ('grp', 'mem'), 'lev'), parts along dimension 1, may hold values from -6 to 6
- precision: float32 [512, 8, 512], P('half', ('grp', 'lev')), parts along dimension 1, may hold values from 0.3 to 3
- row_factor: bfloat16 [512, 256], P('half'), may hold values from -0.375 to 0.375
- col_factor: bfloat16 [512, 256], replicated, may hold values from -0.375 to 0.375
Outputs:
- hessian_product: bfloat16 [256, 48, 4, 256], P('half', ('grp', 'mem'), 'lev'), parts along dimension 1
The draws below stay inside these ranges and needn't reach their ends.
There are 2 independent parts, one for each index of `grp`. The reference program is written for one: setup_inputs(seed, part) draws one part's arguments, and reference() takes and returns one part's arrays. A program takes and returns all parts, laid end to end along the dimension named above; an argument that names none is the same for every part. Nothing has to cross between parts.
All inputs are finite; a program needn't handle non-finite values.
Results may differ from the reference program's by a relative error of at most 0.0095.
Values may be sent and summed in bfloat16 or wider, within the bound.
No kernel may reach another device: no remote copies, remote signals or barrier semaphores. Data moves between devices by JAX's collectives and lax.ppermute only.
A program may use at most 64 MiB of HBM per device.

```python
import math
import jax
import jax.numpy as jnp
from jax import lax

NR = 512
NC = 512
KR = 256
KC = 256
MEMBERS = 24
LEVELS = 4


def levels(key, shape, pieces, low, high):
    gain, own = 1.0, jax.random.fold_in(key, 6)
    for axis_at, shards_of in pieces:
        steps = jnp.exp(jax.random.uniform(jax.random.fold_in(own, axis_at), (shards_of,), jnp.float32, low / len(pieces), high / len(pieces)))
        gain = gain * jnp.repeat(steps, shape[axis_at] // shards_of).reshape([-1 if axis == axis_at else 1 for axis in range(len(shape))])
    return gain


def normal_values(stream_key, dims, width, most, split=(), held_as=jnp.bfloat16):
    gain = levels(stream_key, dims, split, -0.22, 0.18) if split else 1.0
    values = jax.random.normal(stream_key, dims, jnp.float32) * width * gain
    return jnp.minimum(jnp.maximum(values, -most), most).astype(held_as)


def setup_inputs(seed: int = 0, part: int = 0) -> dict:
    seeds = jax.random.split(jax.random.key(seed), 6)
    own_keys = jax.random.split(jax.random.fold_in(seeds[5], part), 6)
    return {
        "anomalies": normal_values(own_keys[0], (NR, MEMBERS, LEVELS, NC), (0.5 * MEMBERS ** -0.25), 3.5, ((0, 2), (1, 4), (2, 2))),
        "control": normal_values(own_keys[1], (KR, MEMBERS, LEVELS, KC), 1.0, 6.0, ((0, 2), (1, 4), (2, 2))),
        "precision": jnp.clip(jnp.exp(math.log(3.0) - 2.3025851 * jax.random.uniform(own_keys[2], (NR, LEVELS, NC), jnp.float32) ** levels(own_keys[2], (NR, LEVELS, NC), ((0, 2), (1, 2)), -0.2, 0.2)), 0.3, 3.0),
        "row_factor": normal_values(seeds[3], (NR, KR), KR ** -0.5, 0.375, ((0, 2),)),
        "col_factor": normal_values(seeds[4], (NC, KC), KC ** -0.5, 0.375),
    }


def one_level(inputs, row_factor, col_factor):
    coeffs, members, weights = inputs
    row_wide = row_factor.astype(jnp.float32)
    col_wide = col_factor.astype(jnp.float32)
    expanded = jnp.einsum('rk,kmc->rmc', row_wide, coeffs.astype(jnp.float32)).astype(jnp.bfloat16)
    fields = jnp.einsum('rmc,nc->rmn', expanded.astype(jnp.float32), col_wide)
    increment = jnp.sum(members.astype(jnp.float32) * fields, axis=1)
    weighted = (weights * increment).astype(jnp.bfloat16)
    scaled = (members.astype(jnp.float32) * weighted.astype(jnp.float32)[:, None, :]).astype(jnp.bfloat16)
    projected = jnp.einsum('rmn,nc->rmc', scaled.astype(jnp.float32), col_wide).astype(jnp.bfloat16)
    summed = jnp.einsum('rk,rmc->kmc', row_wide, projected.astype(jnp.float32))
    return (coeffs.astype(jnp.float32) + summed).astype(jnp.bfloat16)


def reference(anomalies, control, precision, row_factor, col_factor):
    inputs = (jnp.moveaxis(control, 2, 0), jnp.moveaxis(anomalies, 2, 0), jnp.moveaxis(precision, 1, 0))
    result = lax.map(lambda item: one_level(item, row_factor, col_factor), inputs)
    return jnp.moveaxis(result, 0, 2)
```

```python
import jax
import jax.numpy as jnp
from jax import lax
from jax.sharding import PartitionSpec as P


def _swap(x, axis):
    return lax.ppermute(x, axis, [(0, 1), (1, 0)])


def _reduce_scatter_rows(x, axis, size):
    idx = lax.axis_index(axis)
    d = 1
    while d < size:
        half = x.shape[0] // 2
        bit = (idx // d) % 2
        keep = lax.dynamic_slice_in_dim(x, bit * half, half, 0)
        send = lax.dynamic_slice_in_dim(x, (1 - bit) * half, half, 0)
        recv = lax.ppermute(send, axis, [(i, i ^ d) for i in range(size)])
        x = keep + recv
        d *= 2
    return x


def _all_gather_rows(x, axis, size):
    idx = lax.axis_index(axis)
    d = size // 2
    while d >= 1:
        bit = (idx // d) % 2
        recv = lax.ppermute(x, axis, [(i, i ^ d) for i in range(size)])
        lo = jnp.where(bit == 0, x, recv)
        hi = jnp.where(bit == 0, recv, x)
        x = jnp.concatenate([lo, hi], axis=0)
        d //= 2
    return x


def _block_start(axis, size, rows):
    idx = lax.axis_index(axis)
    start = 0
    d, span = 1, rows
    while d < size:
        span //= 2
        start = start + ((idx // d) % 2) * span
        d *= 2
    return start


def local(anomalies, control, precision, row_factor, col_factor, n_mem):
    h = lax.axis_index("half")
    kh = control.shape[0]
    rows = anomalies.shape[0]
    n_lev = anomalies.shape[2]

    ctrl_other = _swap(control, "half")
    rf_own = lax.dynamic_slice_in_dim(row_factor, h * kh, kh, 1)
    rf_other = lax.dynamic_slice_in_dim(row_factor, (1 - h) * kh, kh, 1)
    rf_for_partner = _swap(rf_other, "half")

    pow2 = n_mem & (n_mem - 1) == 0 and rows % n_mem == 0
    blk = rows // n_mem
    start = _block_start("mem", n_mem, rows) if pow2 else 0

    outs = []
    for l in range(n_lev):
        a = anomalies[:, :, l, :]
        c_own = control[:, :, l, :]
        c_oth = ctrl_other[:, :, l, :]
        expanded = (
            jnp.einsum("rk,kmc->rmc", rf_own, c_own, preferred_element_type=jnp.float32)
            + jnp.einsum("rk,kmc->rmc", rf_other, c_oth, preferred_element_type=jnp.float32)
        ).astype(jnp.bfloat16)
        fields = jnp.einsum("rmc,nc->rmn", expanded, col_factor, preferred_element_type=jnp.float32)
        inc = jnp.sum(a.astype(jnp.float32) * fields, axis=1)
        prec = precision[:, l, :]
        if pow2:
            part = _reduce_scatter_rows(inc, "mem", n_mem)
            w_blk = (lax.dynamic_slice_in_dim(prec, start, blk, 0) * part).astype(jnp.bfloat16)
            weighted = _all_gather_rows(w_blk, "mem", n_mem)
        else:
            weighted = (prec * lax.psum(inc, "mem")).astype(jnp.bfloat16)
        scaled = (a.astype(jnp.float32) * weighted.astype(jnp.float32)[:, None, :]).astype(jnp.bfloat16)
        projected = jnp.einsum(
            "rmn,nc->rmc", scaled, col_factor, preferred_element_type=jnp.float32
        ).astype(jnp.bfloat16)
        proj_other = _swap(projected, "half")
        summed = jnp.einsum(
            "rk,rmc->kmc", rf_own, projected, preferred_element_type=jnp.float32
        ) + jnp.einsum("rk,rmc->kmc", rf_for_partner, proj_other, preferred_element_type=jnp.float32)
        outs.append((c_own.astype(jnp.float32) + summed).astype(jnp.bfloat16))
    return jnp.stack(outs, axis=2)


def solution(mesh):
    n_mem = mesh.shape["mem"]

    def f(anomalies, control, precision, row_factor, col_factor):
        return local(anomalies, control, precision, row_factor, col_factor, n_mem)

    return jax.shard_map(
        f,
        mesh=mesh,
        in_specs=(
            P("half", ("grp", "mem"), "lev", None),
            P("half", ("grp", "mem"), "lev", None),
            P("half", ("grp", "lev"), None),
            P("half", None),
            P(),
        ),
        out_specs=P("half", ("grp", "mem"), "lev", None),
        check_vma=False,
    )
```

```python
import jax
import jax.numpy as jnp
from jax import lax
from jax.sharding import PartitionSpec as P


def _swap(x, axis):
    return lax.ppermute(x, axis, [(0, 1), (1, 0)])


def _reduce_scatter_rows(x, axis, size):
    idx = lax.axis_index(axis)
    d = 1
    while d < size:
        half = x.shape[0] // 2
        bit = (idx // d) % 2
        keep = lax.dynamic_slice_in_dim(x, bit * half, half, 0)
        send = lax.dynamic_slice_in_dim(x, (1 - bit) * half, half, 0)
        recv = lax.ppermute(send, axis, [(i, i ^ d) for i in range(size)])
        x = keep + recv
        d *= 2
    return x


def _all_gather_rows(x, axis, size):
    idx = lax.axis_index(axis)
    d = size // 2
    while d >= 1:
        bit = (idx // d) % 2
        recv = lax.ppermute(x, axis, [(i, i ^ d) for i in range(size)])
        lo = jnp.where(bit == 0, x, recv)
        hi = jnp.where(bit == 0, recv, x)
        x = jnp.concatenate([lo, hi], axis=0)
        d //= 2
    return x


def _block_start(axis, size, rows):
    idx = lax.axis_index(axis)
    start = 0
    d, span = 1, rows
    while d < size:
        span //= 2
        start = start + ((idx // d) % 2) * span
        d *= 2
    return start


def local(anomalies, control, precision, row_factor, col_factor, n_mem):
    h = lax.axis_index("half")
    kh = control.shape[0]
    rows = anomalies.shape[0]
    n_lev = anomalies.shape[2]

    anom_t = jnp.transpose(anomalies, (2, 1, 0, 3))
    ctrl_t = jnp.transpose(control, (2, 1, 0, 3))
    prec_t = jnp.transpose(precision, (1, 0, 2))

    ctrl_other = _swap(ctrl_t, "half")
    rf_own = lax.dynamic_slice_in_dim(row_factor, h * kh, kh, 1)
    rf_other = lax.dynamic_slice_in_dim(row_factor, (1 - h) * kh, kh, 1)
    rf_for_partner = _swap(rf_other, "half")

    pow2 = n_mem & (n_mem - 1) == 0 and rows % n_mem == 0
    blk = rows // n_mem
    start = _block_start("mem", n_mem, rows) if pow2 else 0

    outs = []
    for l in range(n_lev):
        a = anom_t[l]
        c_own = ctrl_t[l]
        c_oth = ctrl_other[l]
        expanded = (
            jnp.einsum("rk,mkc->mrc", rf_own, c_own, preferred_element_type=jnp.float32)
            + jnp.einsum("rk,mkc->mrc", rf_other, c_oth, preferred_element_type=jnp.float32)
        ).astype(jnp.bfloat16)
        fields = jnp.einsum("mrc,nc->mrn", expanded, col_factor, preferred_element_type=jnp.float32)
        inc = jnp.sum(a.astype(jnp.float32) * fields, axis=0)
        prec = prec_t[l]
        if pow2:
            part = _reduce_scatter_rows(inc, "mem", n_mem)
            w_blk = (lax.dynamic_slice_in_dim(prec, start, blk, 0) * part).astype(jnp.bfloat16)
            weighted = _all_gather_rows(w_blk, "mem", n_mem)
        else:
            weighted = (prec * lax.psum(inc, "mem")).astype(jnp.bfloat16)
        scaled = (a.astype(jnp.float32) * weighted.astype(jnp.float32)[None]).astype(jnp.bfloat16)
        projected = jnp.einsum(
            "mrn,nc->mrc", scaled, col_factor, preferred_element_type=jnp.float32
        ).astype(jnp.bfloat16)
        proj_other = _swap(projected, "half")
        summed = jnp.einsum(
            "rk,mrc->mkc", rf_own, projected, preferred_element_type=jnp.float32
        ) + jnp.einsum("rk,mrc->mkc", rf_for_partner, proj_other, preferred_element_type=jnp.float32)
        outs.append((c_own.astype(jnp.float32) + summed).astype(jnp.bfloat16))
    return jnp.transpose(jnp.stack(outs, axis=0), (2, 1, 0, 3))


def solution(mesh):
    n_mem = mesh.shape["mem"]

    def f(anomalies, control, precision, row_factor, col_factor):
        return local(anomalies, control, precision, row_factor, col_factor, n_mem)

    return jax.shard_map(
        f,
        mesh=mesh,
        in_specs=(
            P("half", ("grp", "mem"), "lev", None),
            P("half", ("grp", "mem"), "lev", None),
            P("half", ("grp", "lev"), None),
            P("half", None),
            P(),
        ),
        out_specs=P("half", ("grp", "mem"), "lev", None),
        check_vma=False,
    )
```

```python
import jax
import jax.numpy as jnp
from jax import lax
from jax.sharding import PartitionSpec as P


def _swap(x, axis):
    return lax.ppermute(x, axis, [(0, 1), (1, 0)])


def _reduce_scatter_rows(x, axis, size, wire):
    idx = lax.axis_index(axis)
    d = 1
    while d < size:
        half = x.shape[0] // 2
        bit = (idx // d) % 2
        keep = lax.dynamic_slice_in_dim(x, bit * half, half, 0)
        send = lax.dynamic_slice_in_dim(x, (1 - bit) * half, half, 0)
        recv = lax.ppermute(send.astype(wire), axis, [(i, i ^ d) for i in range(size)])
        x = keep + recv.astype(x.dtype)
        d *= 2
    return x


def _all_gather_rows(x, axis, size):
    idx = lax.axis_index(axis)
    d = size // 2
    while d >= 1:
        bit = (idx // d) % 2
        recv = lax.ppermute(x, axis, [(i, i ^ d) for i in range(size)])
        lo = jnp.where(bit == 0, x, recv)
        hi = jnp.where(bit == 0, recv, x)
        x = jnp.concatenate([lo, hi], axis=0)
        d //= 2
    return x


def _block_start(axis, size, rows):
    idx = lax.axis_index(axis)
    start = 0
    d, span = 1, rows
    while d < size:
        span //= 2
        start = start + ((idx // d) % 2) * span
        d *= 2
    return start


def local(anomalies, control, precision, row_factor, col_factor, n_mem):
    h = lax.axis_index("half")
    kh = control.shape[0]
    rows = anomalies.shape[0]
    n_lev = anomalies.shape[2]

    anom_t = jnp.transpose(anomalies, (2, 1, 0, 3))
    ctrl_t = jnp.transpose(control, (2, 1, 0, 3))
    prec_t = jnp.transpose(precision, (1, 0, 2))

    ctrl_other = _swap(ctrl_t, "half")
    rf_own = lax.dynamic_slice_in_dim(row_factor, h * kh, kh, 1)
    rf_other = lax.dynamic_slice_in_dim(row_factor, (1 - h) * kh, kh, 1)
    rf_for_partner = _swap(rf_other, "half")

    pow2 = n_mem & (n_mem - 1) == 0 and rows % n_mem == 0
    blk = rows // n_mem
    start = _block_start("mem", n_mem, rows) if pow2 else 0

    outs = []
    for l in range(n_lev):
        a = anom_t[l]
        c_own = ctrl_t[l]
        c_oth = ctrl_other[l]
        expanded = (
            jnp.einsum("rk,mkc->mrc", rf_own, c_own, preferred_element_type=jnp.float32)
            + jnp.einsum("rk,mkc->mrc", rf_other, c_oth, preferred_element_type=jnp.float32)
        ).astype(jnp.bfloat16)
        fields = jnp.einsum("mrc,nc->mrn", expanded, col_factor, preferred_element_type=jnp.float32)
        inc = jnp.sum(a.astype(jnp.float32) * fields, axis=0)
        prec = prec_t[l]
        if pow2:
            part = _reduce_scatter_rows(inc, "mem", n_mem, jnp.bfloat16)
            w_blk = (lax.dynamic_slice_in_dim(prec, start, blk, 0) * part).astype(jnp.bfloat16)
            weighted = _all_gather_rows(w_blk, "mem", n_mem)
        else:
            weighted = (prec * lax.psum(inc, "mem")).astype(jnp.bfloat16)
        scaled = (a.astype(jnp.float32) * weighted.astype(jnp.float32)[None]).astype(jnp.bfloat16)
        projected = jnp.einsum(
            "mrn,nc->mrc", scaled, col_factor, preferred_element_type=jnp.float32
        ).astype(jnp.bfloat16)
        proj_other = _swap(projected, "half")
        summed = jnp.einsum(
            "rk,mrc->mkc", rf_own, projected, preferred_element_type=jnp.float32
        ) + jnp.einsum("rk,mrc->mkc", rf_for_partner, proj_other, preferred_element_type=jnp.float32)
        outs.append((c_own.astype(jnp.float32) + summed).astype(jnp.bfloat16))
    return jnp.transpose(jnp.stack(outs, axis=0), (2, 1, 0, 3))


def solution(mesh):
    n_mem = mesh.shape["mem"]

    def f(anomalies, control, precision, row_factor, col_factor):
        return local(anomalies, control, precision, row_factor, col_factor, n_mem)

    return jax.shard_map(
        f,
        mesh=mesh,
        in_specs=(
            P("half", ("grp", "mem"), "lev", None),
            P("half", ("grp", "mem"), "lev", None),
            P("half", ("grp", "lev"), None),
            P("half", None),
            P(),
        ),
        out_specs=P("half", ("grp", "mem"), "lev", None),
        check_vma=False,
    )
```

```python
import jax
import jax.numpy as jnp
from jax import lax
from jax.sharding import PartitionSpec as P


def _swap(x, axis):
    return lax.ppermute(x, axis, [(0, 1), (1, 0)])


def _reduce_scatter_rows(x, axis, size, wire):
    idx = lax.axis_index(axis)
    d = 1
    while 2 * d < size:
        half = x.shape[0] // 2
        bit = (idx // d) % 2
        keep = lax.dynamic_slice_in_dim(x, bit * half, half, 0)
        send = lax.dynamic_slice_in_dim(x, (1 - bit) * half, half, 0)
        recv = lax.ppermute(send.astype(wire), axis, [(i, i ^ d) for i in range(size)])
        x = keep + recv.astype(x.dtype)
        d *= 2
    if d < size:
        recv = lax.ppermute(x.astype(wire), axis, [(i, i ^ d) for i in range(size)])
        x = x + recv.astype(x.dtype)
    return x


def _all_gather_rows(x, axis, size):
    idx = lax.axis_index(axis)
    d = size // 4
    while d >= 1:
        bit = (idx // d) % 2
        recv = lax.ppermute(x, axis, [(i, i ^ d) for i in range(size)])
        lo = jnp.where(bit == 0, x, recv)
        hi = jnp.where(bit == 0, recv, x)
        x = jnp.concatenate([lo, hi], axis=0)
        d //= 2
    return x


def _block_start(axis, size, rows):
    idx = lax.axis_index(axis)
    start = 0
    d, span = 1, rows
    while 2 * d < size:
        span //= 2
        start = start + ((idx // d) % 2) * span
        d *= 2
    return start


def local(anomalies, control, precision, row_factor, col_factor, n_mem):
    h = lax.axis_index("half")
    kh = control.shape[0]
    rows = anomalies.shape[0]
    n_lev = anomalies.shape[2]

    anom_t = jnp.transpose(anomalies, (2, 1, 0, 3))
    ctrl_t = jnp.transpose(control, (2, 1, 0, 3))
    prec_t = jnp.transpose(precision, (1, 0, 2))

    ctrl_other = _swap(ctrl_t, "half")
    rf_own = lax.dynamic_slice_in_dim(row_factor, h * kh, kh, 1)
    rf_other = lax.dynamic_slice_in_dim(row_factor, (1 - h) * kh, kh, 1)
    rf_for_partner = _swap(rf_other, "half")

    pow2 = n_mem & (n_mem - 1) == 0 and rows % n_mem == 0
    blk = rows // max(n_mem // 2, 1)
    start = _block_start("mem", n_mem, rows) if pow2 else 0

    outs = []
    for l in range(n_lev):
        a = anom_t[l]
        c_own = ctrl_t[l]
        c_oth = ctrl_other[l]
        expanded = (
            jnp.einsum("rk,mkc->mrc", rf_own, c_own, preferred_element_type=jnp.float32)
            + jnp.einsum("rk,mkc->mrc", rf_other, c_oth, preferred_element_type=jnp.float32)
        ).astype(jnp.bfloat16)
        fields = jnp.einsum("mrc,nc->mrn", expanded, col_factor, preferred_element_type=jnp.float32)
        inc = jnp.sum(a.astype(jnp.float32) * fields, axis=0)
        prec = prec_t[l]
        if pow2:
            part = _reduce_scatter_rows(inc, "mem", n_mem, jnp.bfloat16)
            w_blk = (lax.dynamic_slice_in_dim(prec, start, blk, 0) * part).astype(jnp.bfloat16)
            weighted = _all_gather_rows(w_blk, "mem", n_mem)
        else:
            weighted = (prec * lax.psum(inc, "mem")).astype(jnp.bfloat16)
        scaled = (a.astype(jnp.float32) * weighted.astype(jnp.float32)[None]).astype(jnp.bfloat16)
        projected = jnp.einsum(
            "mrn,nc->mrc", scaled, col_factor, preferred_element_type=jnp.float32
        ).astype(jnp.bfloat16)
        proj_other = _swap(projected, "half")
        summed = jnp.einsum(
            "rk,mrc->mkc", rf_own, projected, preferred_element_type=jnp.float32
        ) + jnp.einsum("rk,mrc->mkc", rf_for_partner, proj_other, preferred_element_type=jnp.float32)
        outs.append((c_own.astype(jnp.float32) + summed).astype(jnp.bfloat16))
    return jnp.transpose(jnp.stack(outs, axis=0), (2, 1, 0, 3))


def solution(mesh):
    n_mem = mesh.shape["mem"]

    def f(anomalies, control, precision, row_factor, col_factor):
        return local(anomalies, control, precision, row_factor, col_factor, n_mem)

    return jax.shard_map(
        f,
        mesh=mesh,
        in_specs=(
            P("half", ("grp", "mem"), "lev", None),
            P("half", ("grp", "mem"), "lev", None),
            P("half", ("grp", "lev"), None),
            P("half", None),
            P(),
        ),
        out_specs=P("half", ("grp", "mem"), "lev", None),
        check_vma=False,
    )
```

```python
import jax
import jax.numpy as jnp
from jax import lax
from jax.sharding import PartitionSpec as P


def _swap(x, axis):
    return lax.ppermute(x, axis, [(0, 1), (1, 0)])


def _reduce_scatter_rows(x, axis, size, wire):
    idx = lax.axis_index(axis)
    d = 1
    while 2 * d < size:
        half = x.shape[0] // 2
        bit = (idx // d) % 2
        keep = lax.dynamic_slice_in_dim(x, bit * half, half, 0)
        send = lax.dynamic_slice_in_dim(x, (1 - bit) * half, half, 0)
        recv = lax.ppermute(send.astype(wire), axis, [(i, i ^ d) for i in range(size)])
        x = keep + recv.astype(x.dtype)
        d *= 2
    if d < size:
        recv = lax.ppermute(x.astype(wire), axis, [(i, i ^ d) for i in range(size)])
        x = x + recv.astype(x.dtype)
    return x


def _all_gather_rows(x, axis, size):
    idx = lax.axis_index(axis)
    d = size // 4
    while d >= 1:
        bit = (idx // d) % 2
        recv = lax.ppermute(x, axis, [(i, i ^ d) for i in range(size)])
        lo = jnp.where(bit == 0, x, recv)
        hi = jnp.where(bit == 0, recv, x)
        x = jnp.concatenate([lo, hi], axis=0)
        d //= 2
    return x


def _block_start(axis, size, rows):
    idx = lax.axis_index(axis)
    start = 0
    d, span = 1, rows
    while 2 * d < size:
        span //= 2
        start = start + ((idx // d) % 2) * span
        d *= 2
    return start


def local(anomalies, control, precision, row_factor, col_factor, n_mem):
    h = lax.axis_index("half")
    kh = control.shape[0]
    rows = anomalies.shape[0]
    n_lev = anomalies.shape[2]

    rf_own = lax.dynamic_slice_in_dim(row_factor, h * kh, kh, 1)
    rf_other = lax.dynamic_slice_in_dim(row_factor, (1 - h) * kh, kh, 1)
    rf_for_partner = _swap(rf_other, "half")

    pow2 = n_mem & (n_mem - 1) == 0 and rows % n_mem == 0
    blk = rows // max(n_mem // 2, 1)
    start = _block_start("mem", n_mem, rows) if pow2 else 0

    outs = []
    for l in range(n_lev):
        a = jnp.transpose(anomalies[:, :, l, :], (1, 0, 2))
        c_own = jnp.transpose(control[:, :, l, :], (1, 0, 2))
        c_oth = _swap(c_own, "half")
        expanded = (
            jnp.einsum("rk,mkc->mrc", rf_own, c_own, preferred_element_type=jnp.float32)
            + jnp.einsum("rk,mkc->mrc", rf_other, c_oth, preferred_element_type=jnp.float32)
        ).astype(jnp.bfloat16)
        fields = jnp.einsum("mrc,nc->mrn", expanded, col_factor, preferred_element_type=jnp.float32)
        inc = jnp.sum(a.astype(jnp.float32) * fields, axis=0)
        prec = precision[:, l, :]
        if pow2:
            part = _reduce_scatter_rows(inc, "mem", n_mem, jnp.bfloat16)
            w_blk = (lax.dynamic_slice_in_dim(prec, start, blk, 0) * part).astype(jnp.bfloat16)
            weighted = _all_gather_rows(w_blk, "mem", n_mem)
        else:
            weighted = (prec * lax.psum(inc, "mem")).astype(jnp.bfloat16)
        scaled = (a.astype(jnp.float32) * weighted.astype(jnp.float32)[None]).astype(jnp.bfloat16)
        projected = jnp.einsum(
            "mrn,nc->mrc", scaled, col_factor, preferred_element_type=jnp.float32
        ).astype(jnp.bfloat16)
        proj_other = _swap(projected, "half")
        summed = jnp.einsum(
            "rk,mrc->mkc", rf_own, projected, preferred_element_type=jnp.float32
        ) + jnp.einsum("rk,mrc->mkc", rf_for_partner, proj_other, preferred_element_type=jnp.float32)
        outs.append(control[:, :, l, :].astype(jnp.float32) + jnp.transpose(summed, (1, 0, 2)))
    return jnp.stack(outs, axis=2).astype(jnp.bfloat16)


def solution(mesh):
    n_mem = mesh.shape["mem"]

    def f(anomalies, control, precision, row_factor, col_factor):
        return local(anomalies, control, precision, row_factor, col_factor, n_mem)

    return jax.shard_map(
        f,
        mesh=mesh,
        in_specs=(
            P("half", ("grp", "mem"), "lev", None),
            P("half", ("grp", "mem"), "lev", None),
            P("half", ("grp", "lev"), None),
            P("half", None),
            P(),
        ),
        out_specs=P("half", ("grp", "mem"), "lev", None),
        check_vma=False,
    )
```

```python
import jax
import jax.numpy as jnp
from jax import lax
from jax.sharding import PartitionSpec as P


def _swap(x, axis):
    return lax.ppermute(x, axis, [(0, 1), (1, 0)])


def _reduce_scatter_rows(x, axis, size, wire):
    idx = lax.axis_index(axis)
    d = 1
    while 2 * d < size:
        half = x.shape[0] // 2
        bit = (idx // d) % 2
        keep = lax.dynamic_slice_in_dim(x, bit * half, half, 0)
        send = lax.dynamic_slice_in_dim(x, (1 - bit) * half, half, 0)
        recv = lax.ppermute(send.astype(wire), axis, [(i, i ^ d) for i in range(size)])
        x = keep + recv.astype(x.dtype)
        d *= 2
    if d < size:
        recv = lax.ppermute(x.astype(wire), axis, [(i, i ^ d) for i in range(size)])
        x = x + recv.astype(x.dtype)
    return x


def _all_gather_rows(x, axis, size):
    idx = lax.axis_index(axis)
    d = size // 4
    while d >= 1:
        bit = (idx // d) % 2
        recv = lax.ppermute(x, axis, [(i, i ^ d) for i in range(size)])
        lo = jnp.where(bit == 0, x, recv)
        hi = jnp.where(bit == 0, recv, x)
        x = jnp.concatenate([lo, hi], axis=0)
        d //= 2
    return x


def _block_start(axis, size, rows):
    idx = lax.axis_index(axis)
    start = 0
    d, span = 1, rows
    while 2 * d < size:
        span //= 2
        start = start + ((idx // d) % 2) * span
        d *= 2
    return start


def local(anomalies, control, precision, row_factor, col_factor, n_mem):
    h = lax.axis_index("half")
    kh = control.shape[0]
    rows = anomalies.shape[0]
    n_lev = anomalies.shape[2]

    anom_t = jnp.transpose(anomalies, (2, 1, 0, 3))
    prec_t = jnp.transpose(precision, (1, 0, 2))

    rf_own = lax.dynamic_slice_in_dim(row_factor, h * kh, kh, 1)
    rf_other = lax.dynamic_slice_in_dim(row_factor, (1 - h) * kh, kh, 1)
    rf_for_partner = _swap(rf_other, "half")
    ctrl_other = _swap(control, "half")
    expanded_all = (
        jnp.einsum("rk,kmlc->lmrc", rf_own, control, preferred_element_type=jnp.float32)
        + jnp.einsum("rk,kmlc->lmrc", rf_other, ctrl_other, preferred_element_type=jnp.float32)
    ).astype(jnp.bfloat16)

    pow2 = n_mem & (n_mem - 1) == 0 and rows % n_mem == 0
    blk = rows // max(n_mem // 2, 1)
    start = _block_start("mem", n_mem, rows) if pow2 else 0

    outs = []
    for l in range(n_lev):
        a = anom_t[l]
        expanded = expanded_all[l]
        fields = jnp.einsum("mrc,nc->mrn", expanded, col_factor, preferred_element_type=jnp.float32)
        inc = jnp.sum(a.astype(jnp.float32) * fields, axis=0)
        prec = prec_t[l]
        if pow2:
            part = _reduce_scatter_rows(inc, "mem", n_mem, jnp.bfloat16)
            w_blk = (lax.dynamic_slice_in_dim(prec, start, blk, 0) * part).astype(jnp.bfloat16)
            weighted = _all_gather_rows(w_blk, "mem", n_mem)
        else:
            weighted = (prec * lax.psum(inc, "mem")).astype(jnp.bfloat16)
        scaled = (a.astype(jnp.float32) * weighted.astype(jnp.float32)[None]).astype(jnp.bfloat16)
        projected = jnp.einsum(
            "mrn,nc->mrc", scaled, col_factor, preferred_element_type=jnp.float32
        ).astype(jnp.bfloat16)
        proj_other = _swap(projected, "half")
        summed = jnp.einsum(
            "rk,mrc->mkc", rf_own, projected, preferred_element_type=jnp.float32
        ) + jnp.einsum("rk,mrc->mkc", rf_for_partner, proj_other, preferred_element_type=jnp.float32)
        outs.append(summed)
    summed_all = jnp.transpose(jnp.stack(outs, axis=0), (2, 1, 0, 3))
    return (control.astype(jnp.float32) + summed_all).astype(jnp.bfloat16)


def solution(mesh):
    n_mem = mesh.shape["mem"]

    def f(anomalies, control, precision, row_factor, col_factor):
        return local(anomalies, control, precision, row_factor, col_factor, n_mem)

    return jax.shard_map(
        f,
        mesh=mesh,
        in_specs=(
            P("half", ("grp", "mem"), "lev", None),
            P("half", ("grp", "mem"), "lev", None),
            P("half", ("grp", "lev"), None),
            P("half", None),
            P(),
        ),
        out_specs=P("half", ("grp", "mem"), "lev", None),
        check_vma=False,
    )
```

```python
import jax
import jax.numpy as jnp
from jax import lax
from jax.sharding import PartitionSpec as P


def _swap(x, axis):
    return lax.ppermute(x, axis, [(0, 1), (1, 0)])


def _reduce_scatter_rows(x, axis, size, wire):
    idx = lax.axis_index(axis)
    d = 1
    while 2 * d < size:
        half = x.shape[0] // 2
        bit = (idx // d) % 2
        keep = lax.dynamic_slice_in_dim(x, bit * half, half, 0)
        send = lax.dynamic_slice_in_dim(x, (1 - bit) * half, half, 0)
        recv = lax.ppermute(send.astype(wire), axis, [(i, i ^ d) for i in range(size)])
        x = keep + recv.astype(x.dtype)
        d *= 2
    if d < size:
        recv = lax.ppermute(x.astype(wire), axis, [(i, i ^ d) for i in range(size)])
        x = x + recv.astype(x.dtype)
    return x


def _all_gather_rows(x, axis, size):
    idx = lax.axis_index(axis)
    d = size // 4
    while d >= 1:
        bit = (idx // d) % 2
        recv = lax.ppermute(x, axis, [(i, i ^ d) for i in range(size)])
        lo = jnp.where(bit == 0, x, recv)
        hi = jnp.where(bit == 0, recv, x)
        x = jnp.concatenate([lo, hi], axis=0)
        d //= 2
    return x


def _block_start(axis, size, rows):
    idx = lax.axis_index(axis)
    start = 0
    d, span = 1, rows
    while 2 * d < size:
        span //= 2
        start = start + ((idx // d) % 2) * span
        d *= 2
    return start


def local(anomalies, control, precision, row_factor, col_factor, n_mem):
    h = lax.axis_index("half")
    kh = control.shape[0]
    rows = anomalies.shape[0]
    n_lev = anomalies.shape[2]

    anom_t = jnp.transpose(anomalies, (2, 1, 0, 3))
    prec_t = jnp.transpose(precision, (1, 0, 2))

    rf_own = lax.dynamic_slice_in_dim(row_factor, h * kh, kh, 1)
    rf_other = lax.dynamic_slice_in_dim(row_factor, (1 - h) * kh, kh, 1)
    ctrl_other = _swap(control, "half")
    expanded_all = (
        jnp.einsum("rk,kmlc->lmrc", rf_own, control, preferred_element_type=jnp.float32)
        + jnp.einsum("rk,kmlc->lmrc", rf_other, ctrl_other, preferred_element_type=jnp.float32)
    ).astype(jnp.bfloat16)

    pow2 = n_mem & (n_mem - 1) == 0 and rows % n_mem == 0
    blk = rows // max(n_mem // 2, 1)
    start = _block_start("mem", n_mem, rows) if pow2 else 0

    outs = []
    for l in range(n_lev):
        a = anom_t[l]
        expanded = expanded_all[l]
        fields = jnp.einsum("mrc,nc->mrn", expanded, col_factor, preferred_element_type=jnp.float32)
        inc = jnp.sum(a.astype(jnp.float32) * fields, axis=0)
        prec = prec_t[l]
        if pow2:
            part = _reduce_scatter_rows(inc, "mem", n_mem, jnp.bfloat16)
            w_blk = (lax.dynamic_slice_in_dim(prec, start, blk, 0) * part).astype(jnp.bfloat16)
            weighted = _all_gather_rows(w_blk, "mem", n_mem)
        else:
            weighted = (prec * lax.psum(inc, "mem")).astype(jnp.bfloat16)
        scaled = (a.astype(jnp.float32) * weighted.astype(jnp.float32)[None]).astype(jnp.bfloat16)
        projected = jnp.einsum(
            "mrn,nc->mrc", scaled, col_factor, preferred_element_type=jnp.float32
        ).astype(jnp.bfloat16)
        for_partner = jnp.einsum("rk,mrc->mkc", rf_other, projected, preferred_element_type=jnp.float32)
        from_partner = _swap(for_partner.astype(jnp.bfloat16), "half")
        summed = jnp.einsum(
            "rk,mrc->mkc", rf_own, projected, preferred_element_type=jnp.float32
        ) + from_partner.astype(jnp.float32)
        outs.append(summed)
    summed_all = jnp.transpose(jnp.stack(outs, axis=0), (2, 1, 0, 3))
    return (control.astype(jnp.float32) + summed_all).astype(jnp.bfloat16)


def solution(mesh):
    n_mem = mesh.shape["mem"]

    def f(anomalies, control, precision, row_factor, col_factor):
        return local(anomalies, control, precision, row_factor, col_factor, n_mem)

    return jax.shard_map(
        f,
        mesh=mesh,
        in_specs=(
            P("half", ("grp", "mem"), "lev", None),
            P("half", ("grp", "mem"), "lev", None),
            P("half", ("grp", "lev"), None),
            P("half", None),
            P(),
        ),
        out_specs=P("half", ("grp", "mem"), "lev", None),
        check_vma=False,
    )
```

```python
import jax
import jax.numpy as jnp
from jax import lax
from jax.sharding import PartitionSpec as P


def _swap(x, axis):
    return lax.ppermute(x, axis, [(0, 1), (1, 0)])


def _pairs(size, d):
    return [(i, i ^ d) for i in range(size)]


def _reduce_scatter_rows(x, axis, size, dists, wire):
    idx = lax.axis_index(axis)
    for d in dists[:-1]:
        half = x.shape[0] // 2
        bit = (idx // d) % 2
        keep = lax.dynamic_slice_in_dim(x, bit * half, half, 0)
        send = lax.dynamic_slice_in_dim(x, (1 - bit) * half, half, 0)
        recv = lax.ppermute(send.astype(wire), axis, _pairs(size, d))
        x = keep + recv.astype(x.dtype)
    if dists:
        recv = lax.ppermute(x.astype(wire), axis, _pairs(size, dists[-1]))
        x = x + recv.astype(x.dtype)
    return x


def _all_gather_rows(x, axis, size, dists):
    idx = lax.axis_index(axis)
    for d in reversed(dists[:-1]):
        bit = (idx // d) % 2
        recv = lax.ppermute(x, axis, _pairs(size, d))
        lo = jnp.where(bit == 0, x, recv)
        hi = jnp.where(bit == 0, recv, x)
        x = jnp.concatenate([lo, hi], axis=0)
    return x


def _block_start(axis, dists, rows):
    idx = lax.axis_index(axis)
    start = 0
    span = rows
    for d in dists[:-1]:
        span //= 2
        start = start + ((idx // d) % 2) * span
    return start


def local(anomalies, control, precision, row_factor, col_factor, n_mem):
    h = lax.axis_index("half")
    kh = control.shape[0]
    rows = anomalies.shape[0]
    n_lev = anomalies.shape[2]

    anom_t = jnp.transpose(anomalies, (2, 1, 0, 3))
    prec_t = jnp.transpose(precision, (1, 0, 2))

    rf_own = lax.dynamic_slice_in_dim(row_factor, h * kh, kh, 1)
    rf_other = lax.dynamic_slice_in_dim(row_factor, (1 - h) * kh, kh, 1)
    rf_for_partner = _swap(rf_other, "half")
    ctrl_other = _swap(control, "half")
    expanded_all = (
        jnp.einsum("rk,kmlc->lmrc", rf_own, control, preferred_element_type=jnp.float32)
        + jnp.einsum("rk,kmlc->lmrc", rf_other, ctrl_other, preferred_element_type=jnp.float32)
    ).astype(jnp.bfloat16)

    pow2 = n_mem & (n_mem - 1) == 0 and rows % n_mem == 0
    blk = rows // max(n_mem // 2, 1)
    near_first = []
    d = 1
    while d < n_mem:
        near_first.append(d)
        d *= 2
    far_first = near_first[::-1]

    outs = []
    for l in range(n_lev):
        a = anom_t[l]
        expanded = expanded_all[l]
        fields = jnp.einsum("mrc,nc->mrn", expanded, col_factor, preferred_element_type=jnp.float32)
        inc = jnp.sum(a.astype(jnp.float32) * fields, axis=0)
        prec = prec_t[l]
        if pow2:
            dists = near_first if l % 2 == 0 else far_first
            part = _reduce_scatter_rows(inc, "mem", n_mem, dists, jnp.bfloat16)
            start = _block_start("mem", dists, rows)
            w_blk = (lax.dynamic_slice_in_dim(prec, start, blk, 0) * part).astype(jnp.bfloat16)
            weighted = _all_gather_rows(w_blk, "mem", n_mem, dists)
        else:
            weighted = (prec * lax.psum(inc, "mem")).astype(jnp.bfloat16)
        scaled = (a.astype(jnp.float32) * weighted.astype(jnp.float32)[None]).astype(jnp.bfloat16)
        projected = jnp.einsum(
            "mrn,nc->mrc", scaled, col_factor, preferred_element_type=jnp.float32
        ).astype(jnp.bfloat16)
        proj_other = _swap(projected, "half")
        summed = jnp.einsum(
            "rk,mrc->mkc", rf_own, projected, preferred_element_type=jnp.float32
        ) + jnp.einsum("rk,mrc->mkc", rf_for_partner, proj_other, preferred_element_type=jnp.float32)
        outs.append(summed)
    summed_all = jnp.transpose(jnp.stack(outs, axis=0), (2, 1, 0, 3))
    return (control.astype(jnp.float32) + summed_all).astype(jnp.bfloat16)


def solution(mesh):
    n_mem = mesh.shape["mem"]

    def f(anomalies, control, precision, row_factor, col_factor):
        return local(anomalies, control, precision, row_factor, col_factor, n_mem)

    return jax.shard_map(
        f,
        mesh=mesh,
        in_specs=(
            P("half", ("grp", "mem"), "lev", None),
            P("half", ("grp", "mem"), "lev", None),
            P("half", ("grp", "lev"), None),
            P("half", None),
            P(),
        ),
        out_specs=P("half", ("grp", "mem"), "lev", None),
        check_vma=False,
    )
```

```python
import jax
import jax.numpy as jnp
from jax import lax
from jax.sharding import PartitionSpec as P


def _swap(x, axis):
    return lax.ppermute(x, axis, [(0, 1), (1, 0)])


def _pairs(size, d):
    return [(i, i ^ d) for i in range(size)]


def _reduce_scatter_rows(x, axis, size, dists, wire):
    idx = lax.axis_index(axis)
    for d in dists[:-1]:
        half = x.shape[0] // 2
        bit = (idx // d) % 2
        keep = lax.dynamic_slice_in_dim(x, bit * half, half, 0)
        send = lax.dynamic_slice_in_dim(x, (1 - bit) * half, half, 0)
        recv = lax.ppermute(send.astype(wire), axis, _pairs(size, d))
        x = keep + recv.astype(x.dtype)
    if dists:
        recv = lax.ppermute(x.astype(wire), axis, _pairs(size, dists[-1]))
        x = x + recv.astype(x.dtype)
    return x


def _all_gather_pieces(x, start, axis, size, dists):
    idx = lax.axis_index(axis)
    pieces = [(x, start)]
    span = x.shape[0]
    for d in reversed(dists[:-1]):
        bit = (idx // d) % 2
        recv = lax.ppermute(x, axis, _pairs(size, d))
        pieces.append((recv, start + (1 - 2 * bit) * span))
        lo = jnp.where(bit == 0, x, recv)
        hi = jnp.where(bit == 0, recv, x)
        x = jnp.concatenate([lo, hi], axis=0)
        start = start - bit * span
        span *= 2
    return pieces


def _block_start(axis, dists, rows):
    idx = lax.axis_index(axis)
    start = 0
    span = rows
    for d in dists[:-1]:
        span //= 2
        start = start + ((idx // d) % 2) * span
    return start


def local(anomalies, control, precision, row_factor, col_factor, n_mem):
    h = lax.axis_index("half")
    kh = control.shape[0]
    rows = anomalies.shape[0]
    n_lev = anomalies.shape[2]

    anom_t = jnp.transpose(anomalies, (2, 1, 0, 3))
    prec_t = jnp.transpose(precision, (1, 0, 2))

    rf_own = lax.dynamic_slice_in_dim(row_factor, h * kh, kh, 1)
    rf_other = lax.dynamic_slice_in_dim(row_factor, (1 - h) * kh, kh, 1)
    rf_for_partner = _swap(rf_other, "half")
    ctrl_other = _swap(control, "half")
    expanded_all = (
        jnp.einsum("rk,kmlc->lmrc", rf_own, control, preferred_element_type=jnp.float32)
        + jnp.einsum("rk,kmlc->lmrc", rf_other, ctrl_other, preferred_element_type=jnp.float32)
    ).astype(jnp.bfloat16)

    pow2 = n_mem & (n_mem - 1) == 0 and rows % n_mem == 0
    blk = rows // max(n_mem // 2, 1)
    near_first = []
    d = 1
    while d < n_mem:
        near_first.append(d)
        d *= 2

    outs = []
    for l in range(n_lev):
        a = anom_t[l]
        expanded = expanded_all[l]
        fields = jnp.einsum("mrc,nc->mrn", expanded, col_factor, preferred_element_type=jnp.float32)
        inc = jnp.sum(a.astype(jnp.float32) * fields, axis=0)
        prec = prec_t[l]
        if pow2:
            dists = near_first
            part = _reduce_scatter_rows(inc, "mem", n_mem, dists, jnp.bfloat16)
            start = _block_start("mem", dists, rows)
            w_blk = (lax.dynamic_slice_in_dim(prec, start, blk, 0) * part).astype(jnp.bfloat16)
            pieces = _all_gather_pieces(w_blk, start, "mem", n_mem, dists)
        else:
            weighted = (prec * lax.psum(inc, "mem")).astype(jnp.bfloat16)
            pieces = [(weighted, 0)]
        summed = None
        for w, off in pieces:
            n = w.shape[0]
            a_p = lax.dynamic_slice_in_dim(a, off, n, 1)
            scaled = (a_p.astype(jnp.float32) * w.astype(jnp.float32)[None]).astype(jnp.bfloat16)
            projected = jnp.einsum(
                "mrn,nc->mrc", scaled, col_factor, preferred_element_type=jnp.float32
            ).astype(jnp.bfloat16)
            proj_other = _swap(projected, "half")
            part_sum = jnp.einsum(
                "rk,mrc->mkc", lax.dynamic_slice_in_dim(rf_own, off, n, 0), projected,
                preferred_element_type=jnp.float32,
            ) + jnp.einsum(
                "rk,mrc->mkc", lax.dynamic_slice_in_dim(rf_for_partner, off, n, 0), proj_other,
                preferred_element_type=jnp.float32,
            )
            summed = part_sum if summed is None else summed + part_sum
        outs.append(summed)
    summed_all = jnp.transpose(jnp.stack(outs, axis=0), (2, 1, 0, 3))
    return (control.astype(jnp.float32) + summed_all).astype(jnp.bfloat16)


def solution(mesh):
    n_mem = mesh.shape["mem"]

    def f(anomalies, control, precision, row_factor, col_factor):
        return local(anomalies, control, precision, row_factor, col_factor, n_mem)

    return jax.shard_map(
        f,
        mesh=mesh,
        in_specs=(
            P("half", ("grp", "mem"), "lev", None),
            P("half", ("grp", "mem"), "lev", None),
            P("half", ("grp", "lev"), None),
            P("half", None),
            P(),
        ),
        out_specs=P("half", ("grp", "mem"), "lev", None),
        check_vma=False,
    )
```

```python
import jax
import jax.numpy as jnp
from jax import lax
from jax.sharding import PartitionSpec as P


def _swap(x, axis):
    return lax.ppermute(x, axis, [(0, 1), (1, 0)])


def _reduce_scatter_rows(x, axis, size, wire):
    idx = lax.axis_index(axis)
    d = 1
    while 2 * d < size:
        half = x.shape[0] // 2
        bit = (idx // d) % 2
        keep = lax.dynamic_slice_in_dim(x, bit * half, half, 0)
        send = lax.dynamic_slice_in_dim(x, (1 - bit) * half, half, 0)
        recv = lax.ppermute(send.astype(wire), axis, [(i, i ^ d) for i in range(size)])
        x = keep + recv.astype(x.dtype)
        d *= 2
    if d < size:
        recv = lax.ppermute(x.astype(wire), axis, [(i, i ^ d) for i in range(size)])
        x = x + recv.astype(x.dtype)
    return x


def _all_gather_rows(x, axis, size):
    idx = lax.axis_index(axis)
    d = size // 4
    while d >= 1:
        bit = (idx // d) % 2
        recv = lax.ppermute(x, axis, [(i, i ^ d) for i in range(size)])
        lo = jnp.where(bit == 0, x, recv)
        hi = jnp.where(bit == 0, recv, x)
        x = jnp.concatenate([lo, hi], axis=0)
        d //= 2
    return x


def _block_start(axis, size, rows):
    idx = lax.axis_index(axis)
    start = 0
    d, span = 1, rows
    while 2 * d < size:
        span //= 2
        start = start + ((idx // d) % 2) * span
        d *= 2
    return start


def local(anomalies, control, precision, row_factor, col_factor, n_mem):
    h = lax.axis_index("half")
    kh = control.shape[0]
    rows = anomalies.shape[0]
    n_lev = anomalies.shape[2]

    anom_t = jnp.transpose(anomalies, (2, 1, 0, 3))
    prec_t = jnp.transpose(precision, (1, 0, 2))

    rf_own = lax.dynamic_slice_in_dim(row_factor, h * kh, kh, 1)
    rf_other = lax.dynamic_slice_in_dim(row_factor, (1 - h) * kh, kh, 1)
    rf_for_partner = _swap(rf_other, "half")
    ctrl_other = _swap(control, "half")
    expanded_all = (
        jnp.einsum("rk,kmlc->lmrc", rf_own, control, preferred_element_type=jnp.float32)
        + jnp.einsum("rk,kmlc->lmrc", rf_other, ctrl_other, preferred_element_type=jnp.float32)
    ).astype(jnp.bfloat16)

    pow2 = n_mem & (n_mem - 1) == 0 and rows % n_mem == 0
    blk = rows // max(n_mem // 2, 1)
    start = _block_start("mem", n_mem, rows) if pow2 else 0

    outs = []
    for l in range(n_lev):
        a = anom_t[l]
        expanded = expanded_all[l]
        fields = jnp.einsum("mrc,nc->mrn", expanded, col_factor, preferred_element_type=jnp.float32)
        inc = jnp.sum(a.astype(jnp.float32) * fields, axis=0)
        prec = prec_t[l]
        if pow2:
            part = _reduce_scatter_rows(inc, "mem", n_mem, jnp.bfloat16)
            w_blk = (lax.dynamic_slice_in_dim(prec, start, blk, 0) * part).astype(jnp.bfloat16)
            weighted = _all_gather_rows(w_blk, "mem", n_mem)
        else:
            weighted = (prec * lax.psum(inc, "mem")).astype(jnp.bfloat16)
        scaled = (a.astype(jnp.float32) * weighted.astype(jnp.float32)[None]).astype(jnp.bfloat16)
        projected = jnp.einsum(
            "mrn,nc->mrc", scaled, col_factor, preferred_element_type=jnp.float32
        ).astype(jnp.bfloat16)
        n_m = projected.shape[0]
        mh = n_m // 2
        chunks = [(0, mh), (mh, n_m)] if mh > 0 else [(0, n_m)]
        summed = jnp.einsum("rk,mrc->kmc", rf_own, projected, preferred_element_type=jnp.float32)
        other = []
        for lo, hi in chunks:
            proj_other = _swap(projected[lo:hi], "half")
            other.append(jnp.einsum(
                "rk,mrc->kmc", rf_for_partner, proj_other, preferred_element_type=jnp.float32
            ))
        summed = summed + jnp.concatenate(other, axis=1)
        outs.append(control[:, :, l, :].astype(jnp.float32) + summed)
    return jnp.stack(outs, axis=2).astype(jnp.bfloat16)


def solution(mesh):
    n_mem = mesh.shape["mem"]

    def f(anomalies, control, precision, row_factor, col_factor):
        return local(anomalies, control, precision, row_factor, col_factor, n_mem)

    return jax.shard_map(
        f,
        mesh=mesh,
        in_specs=(
            P("half", ("grp", "mem"), "lev", None),
            P("half", ("grp", "mem"), "lev", None),
            P("half", ("grp", "lev"), None),
            P("half", None),
            P(),
        ),
        out_specs=P("half", ("grp", "mem"), "lev", None),
        check_vma=False,
    )
```

```python
import jax
import jax.numpy as jnp
from jax import lax
from jax.sharding import PartitionSpec as P


def _swap(x, axis):
    return lax.ppermute(x, axis, [(0, 1), (1, 0)])


def _reduce_scatter_rows(x, axis, size, wire):
    idx = lax.axis_index(axis)
    d = 1
    while 2 * d < size:
        half = x.shape[0] // 2
        bit = (idx // d) % 2
        keep = lax.dynamic_slice_in_dim(x, bit * half, half, 0)
        send = lax.dynamic_slice_in_dim(x, (1 - bit) * half, half, 0)
        recv = lax.ppermute(send.astype(wire), axis, [(i, i ^ d) for i in range(size)])
        x = keep + recv.astype(x.dtype)
        d *= 2
    if d < size:
        recv = lax.ppermute(x.astype(wire), axis, [(i, i ^ d) for i in range(size)])
        x = x + recv.astype(x.dtype)
    return x


def _all_gather_rows(x, axis, size):
    idx = lax.axis_index(axis)
    d = size // 4
    while d >= 1:
        bit = (idx // d) % 2
        recv = lax.ppermute(x, axis, [(i, i ^ d) for i in range(size)])
        lo = jnp.where(bit == 0, x, recv)
        hi = jnp.where(bit == 0, recv, x)
        x = jnp.concatenate([lo, hi], axis=0)
        d //= 2
    return x


def _block_start(axis, size, rows):
    idx = lax.axis_index(axis)
    start = 0
    d, span = 1, rows
    while 2 * d < size:
        span //= 2
        start = start + ((idx // d) % 2) * span
        d *= 2
    return start


def local(anomalies, control, precision, row_factor, col_factor, n_mem):
    h = lax.axis_index("half")
    kh = control.shape[0]
    rows = anomalies.shape[0]
    n_lev = anomalies.shape[2]

    anom_t = jnp.transpose(anomalies, (2, 1, 0, 3))
    prec_t = jnp.transpose(precision, (1, 0, 2))

    rf_own = lax.dynamic_slice_in_dim(row_factor, h * kh, kh, 1)
    rf_other = lax.dynamic_slice_in_dim(row_factor, (1 - h) * kh, kh, 1)
    rf_for_partner = _swap(rf_other, "half")
    ctrl_other = _swap(control, "half")
    expanded_all = (
        jnp.einsum("rk,kmlc->lmrc", rf_own, control, preferred_element_type=jnp.float32)
        + jnp.einsum("rk,kmlc->lmrc", rf_other, ctrl_other, preferred_element_type=jnp.float32)
    ).astype(jnp.bfloat16)

    pow2 = n_mem & (n_mem - 1) == 0 and rows % n_mem == 0
    blk = rows // max(n_mem // 2, 1)
    start = _block_start("mem", n_mem, rows) if pow2 else 0

    outs = []
    for l in range(n_lev):
        a = anom_t[l]
        expanded = expanded_all[l]
        fields = jnp.einsum("mrc,nc->mrn", expanded, col_factor, preferred_element_type=jnp.float32)
        inc = jnp.sum(a.astype(jnp.float32) * fields, axis=0)
        prec = prec_t[l]
        if pow2:
            part = _reduce_scatter_rows(inc, "mem", n_mem, jnp.bfloat16)
            w_blk = (lax.dynamic_slice_in_dim(prec, start, blk, 0) * part).astype(jnp.bfloat16)
            weighted = _all_gather_rows(w_blk, "mem", n_mem)
        else:
            weighted = (prec * lax.psum(inc, "mem")).astype(jnp.bfloat16)
        scaled = (a.astype(jnp.float32) * weighted.astype(jnp.float32)[None]).astype(jnp.bfloat16)
        projected = jnp.einsum(
            "mrn,nc->mrc", scaled, col_factor, preferred_element_type=jnp.float32
        ).astype(jnp.bfloat16)
        n_m = projected.shape[0]
        mh = n_m // 2
        chunks = [(0, mh), (mh, n_m)] if mh > 0 else [(0, n_m)]
        summed = jnp.einsum("rk,mrc->kmc", rf_own, projected, preferred_element_type=jnp.float32)
        other = []
        for lo, hi in chunks:
            proj_other = _swap(projected[lo:hi], "half")
            other.append(jnp.einsum(
                "rk,mrc->kmc", rf_for_partner, proj_other, preferred_element_type=jnp.float32
            ))
        summed = summed + jnp.concatenate(other, axis=1)
        outs.append(summed)
    return (control.astype(jnp.float32) + jnp.stack(outs, axis=2)).astype(jnp.bfloat16)


def solution(mesh):
    n_mem = mesh.shape["mem"]

    def f(anomalies, control, precision, row_factor, col_factor):
        return local(anomalies, control, precision, row_factor, col_factor, n_mem)

    return jax.shard_map(
        f,
        mesh=mesh,
        in_specs=(
            P("half", ("grp", "mem"), "lev", None),
            P("half", ("grp", "mem"), "lev", None),
            P("half", ("grp", "lev"), None),
            P("half", None),
            P(),
        ),
        out_specs=P("half", ("grp", "mem"), "lev", None),
        check_vma=False,
    )
```

```python
import jax
import jax.numpy as jnp
from jax import lax
from jax.sharding import PartitionSpec as P


def _swap(x, axis):
    return lax.ppermute(x, axis, [(0, 1), (1, 0)])


def _reduce_scatter_rows(x, axis, size, wire):
    idx = lax.axis_index(axis)
    d = 1
    while 2 * d < size:
        half = x.shape[0] // 2
        bit = (idx // d) % 2
        keep = lax.dynamic_slice_in_dim(x, bit * half, half, 0)
        send = lax.dynamic_slice_in_dim(x, (1 - bit) * half, half, 0)
        recv = lax.ppermute(send.astype(wire), axis, [(i, i ^ d) for i in range(size)])
        x = keep + recv.astype(x.dtype)
        d *= 2
    if d < size:
        recv = lax.ppermute(x.astype(wire), axis, [(i, i ^ d) for i in range(size)])
        x = x + recv.astype(x.dtype)
    return x


def _all_gather_rows(x, axis, size):
    idx = lax.axis_index(axis)
    d = size // 4
    while d >= 1:
        bit = (idx // d) % 2
        recv = lax.ppermute(x, axis, [(i, i ^ d) for i in range(size)])
        lo = jnp.where(bit == 0, x, recv)
        hi = jnp.where(bit == 0, recv, x)
        x = jnp.concatenate([lo, hi], axis=0)
        d //= 2
    return x


def _block_start(axis, size, rows):
    idx = lax.axis_index(axis)
    start = 0
    d, span = 1, rows
    while 2 * d < size:
        span //= 2
        start = start + ((idx // d) % 2) * span
        d *= 2
    return start


def local(anomalies, control, precision, row_factor, col_factor, n_mem):
    h = lax.axis_index("half")
    kh = control.shape[0]
    rows = anomalies.shape[0]
    n_lev = anomalies.shape[2]

    anom_t = jnp.transpose(anomalies, (2, 1, 0, 3))
    prec_t = jnp.transpose(precision, (1, 0, 2))

    rf_own = lax.dynamic_slice_in_dim(row_factor, h * kh, kh, 1)
    rf_other = lax.dynamic_slice_in_dim(row_factor, (1 - h) * kh, kh, 1)
    rf_for_partner = _swap(rf_other, "half")
    ctrl_t = jnp.transpose(control, (2, 1, 0, 3))

    pow2 = n_mem & (n_mem - 1) == 0 and rows % n_mem == 0
    blk = rows // max(n_mem // 2, 1)
    start = _block_start("mem", n_mem, rows) if pow2 else 0

    outs = []
    for l in range(n_lev):
        a = anom_t[l]
        c_own = ctrl_t[l]
        c_oth = _swap(c_own, "half")
        expanded = (
            jnp.einsum("rk,mkc->mrc", rf_own, c_own, preferred_element_type=jnp.float32)
            + jnp.einsum("rk,mkc->mrc", rf_other, c_oth, preferred_element_type=jnp.float32)
        ).astype(jnp.bfloat16)
        fields = jnp.einsum("mrc,nc->mrn", expanded, col_factor, preferred_element_type=jnp.float32)
        inc = jnp.sum(a.astype(jnp.float32) * fields, axis=0)
        prec = prec_t[l]
        if pow2:
            part = _reduce_scatter_rows(inc, "mem", n_mem, jnp.bfloat16)
            w_blk = (lax.dynamic_slice_in_dim(prec, start, blk, 0) * part).astype(jnp.bfloat16)
            weighted = _all_gather_rows(w_blk, "mem", n_mem)
        else:
            weighted = (prec * lax.psum(inc, "mem")).astype(jnp.bfloat16)
        scaled = (a.astype(jnp.float32) * weighted.astype(jnp.float32)[None]).astype(jnp.bfloat16)
        projected = jnp.einsum(
            "mrn,nc->mrc", scaled, col_factor, preferred_element_type=jnp.float32
        ).astype(jnp.bfloat16)
        n_m = projected.shape[0]
        mh = n_m // 2
        chunks = [(0, mh), (mh, n_m)] if mh > 0 else [(0, n_m)]
        summed = jnp.einsum("rk,mrc->kmc", rf_own, projected, preferred_element_type=jnp.float32)
        other = []
        for lo, hi in chunks:
            proj_other = _swap(projected[lo:hi], "half")
            other.append(jnp.einsum(
                "rk,mrc->kmc", rf_for_partner, proj_other, preferred_element_type=jnp.float32
            ))
        summed = summed + jnp.concatenate(other, axis=1)
        outs.append(summed)
    return (control.astype(jnp.float32) + jnp.stack(outs, axis=2)).astype(jnp.bfloat16)


def solution(mesh):
    n_mem = mesh.shape["mem"]

    def f(anomalies, control, precision, row_factor, col_factor):
        return local(anomalies, control, precision, row_factor, col_factor, n_mem)

    return jax.shard_map(
        f,
        mesh=mesh,
        in_specs=(
            P("half", ("grp", "mem"), "lev", None),
            P("half", ("grp", "mem"), "lev", None),
            P("half", ("grp", "lev"), None),
            P("half", None),
            P(),
        ),
        out_specs=P("half", ("grp", "mem"), "lev", None),
        check_vma=False,
    )
```

```python
import jax
import jax.numpy as jnp
from jax import lax
from jax.sharding import PartitionSpec as P


def _swap(x, axis):
    return lax.ppermute(x, axis, [(0, 1), (1, 0)])


def _reduce_scatter_rows(x, axis, size, wire):
    idx = lax.axis_index(axis)
    d = 1
    while 2 * d < size:
        half = x.shape[0] // 2
        bit = (idx // d) % 2
        keep = lax.dynamic_slice_in_dim(x, bit * half, half, 0)
        send = lax.dynamic_slice_in_dim(x, (1 - bit) * half, half, 0)
        recv = lax.ppermute(send.astype(wire), axis, [(i, i ^ d) for i in range(size)])
        x = keep + recv.astype(x.dtype)
        d *= 2
    if d < size:
        recv = lax.ppermute(x.astype(wire), axis, [(i, i ^ d) for i in range(size)])
        x = x + recv.astype(x.dtype)
    return x


def _all_gather_rows(x, axis, size):
    idx = lax.axis_index(axis)
    d = size // 4
    while d >= 1:
        bit = (idx // d) % 2
        recv = lax.ppermute(x, axis, [(i, i ^ d) for i in range(size)])
        lo = jnp.where(bit == 0, x, recv)
        hi = jnp.where(bit == 0, recv, x)
        x = jnp.concatenate([lo, hi], axis=0)
        d //= 2
    return x


def _block_start(axis, size, rows):
    idx = lax.axis_index(axis)
    start = 0
    d, span = 1, rows
    while 2 * d < size:
        span //= 2
        start = start + ((idx // d) % 2) * span
        d *= 2
    return start


def local(anomalies, control, precision, row_factor, col_factor, n_mem):
    h = lax.axis_index("half")
    kh = control.shape[0]
    rows = anomalies.shape[0]
    n_lev = anomalies.shape[2]

    anom_t = jnp.transpose(anomalies, (2, 1, 0, 3))
    prec_t = jnp.transpose(precision, (1, 0, 2))

    rf_own = lax.dynamic_slice_in_dim(row_factor, h * kh, kh, 1)
    rf_other = lax.dynamic_slice_in_dim(row_factor, (1 - h) * kh, kh, 1)
    rf_for_partner = _swap(rf_other, "half")

    pow2 = n_mem & (n_mem - 1) == 0 and rows % n_mem == 0
    blk = rows // max(n_mem // 2, 1)
    start = _block_start("mem", n_mem, rows) if pow2 else 0

    outs = []
    for l in range(n_lev):
        a = anom_t[l]
        c_own = control[:, :, l, :]
        c_oth = _swap(c_own, "half")
        expanded = (
            jnp.einsum("rk,kmc->mrc", rf_own, c_own, preferred_element_type=jnp.float32)
            + jnp.einsum("rk,kmc->mrc", rf_other, c_oth, preferred_element_type=jnp.float32)
        ).astype(jnp.bfloat16)
        fields = jnp.einsum("mrc,nc->mrn", expanded, col_factor, preferred_element_type=jnp.float32)
        inc = jnp.sum(a.astype(jnp.float32) * fields, axis=0)
        prec = prec_t[l]
        if pow2:
            part = _reduce_scatter_rows(inc, "mem", n_mem, jnp.bfloat16)
            w_blk = (lax.dynamic_slice_in_dim(prec, start, blk, 0) * part).astype(jnp.bfloat16)
            weighted = _all_gather_rows(w_blk, "mem", n_mem)
        else:
            weighted = (prec * lax.psum(inc, "mem")).astype(jnp.bfloat16)
        scaled = (a.astype(jnp.float32) * weighted.astype(jnp.float32)[None]).astype(jnp.bfloat16)
        projected = jnp.einsum(
            "mrn,nc->mrc", scaled, col_factor, preferred_element_type=jnp.float32
        ).astype(jnp.bfloat16)
        n_m = projected.shape[0]
        mh = n_m // 2
        chunks = [(0, mh), (mh, n_m)] if mh > 0 else [(0, n_m)]
        summed = jnp.einsum("rk,mrc->kmc", rf_own, projected, preferred_element_type=jnp.float32)
        other = []
        for lo, hi in chunks:
            proj_other = _swap(projected[lo:hi], "half")
            other.append(jnp.einsum(
                "rk,mrc->kmc", rf_for_partner, proj_other, preferred_element_type=jnp.float32
            ))
        summed = summed + jnp.concatenate(other, axis=1)
        outs.append(summed)
    return (control.astype(jnp.float32) + jnp.stack(outs, axis=2)).astype(jnp.bfloat16)


def solution(mesh):
    n_mem = mesh.shape["mem"]

    def f(anomalies, control, precision, row_factor, col_factor):
        return local(anomalies, control, precision, row_factor, col_factor, n_mem)

    return jax.shard_map(
        f,
        mesh=mesh,
        in_specs=(
            P("half", ("grp", "mem"), "lev", None),
            P("half", ("grp", "mem"), "lev", None),
            P("half", ("grp", "lev"), None),
            P("half", None),
            P(),
        ),
        out_specs=P("half", ("grp", "mem"), "lev", None),
        check_vma=False,
    )
```

```python
import jax
import jax.numpy as jnp
from jax import lax
from jax.sharding import PartitionSpec as P


def _swap(x, axis):
    return lax.ppermute(x, axis, [(0, 1), (1, 0)])


def _reduce_scatter_rows(x, axis, size, wire):
    idx = lax.axis_index(axis)
    d = 1
    while 2 * d < size:
        half = x.shape[0] // 2
        bit = (idx // d) % 2
        keep = lax.dynamic_slice_in_dim(x, bit * half, half, 0)
        send = lax.dynamic_slice_in_dim(x, (1 - bit) * half, half, 0)
        recv = lax.ppermute(send.astype(wire), axis, [(i, i ^ d) for i in range(size)])
        x = keep + recv.astype(x.dtype)
        d *= 2
    if d < size:
        recv = lax.ppermute(x.astype(wire), axis, [(i, i ^ d) for i in range(size)])
        x = x + recv.astype(x.dtype)
    return x


def _all_gather_rows(x, axis, size):
    idx = lax.axis_index(axis)
    d = size // 4
    while d >= 1:
        bit = (idx // d) % 2
        recv = lax.ppermute(x, axis, [(i, i ^ d) for i in range(size)])
        lo = jnp.where(bit == 0, x, recv)
        hi = jnp.where(bit == 0, recv, x)
        x = jnp.concatenate([lo, hi], axis=0)
        d //= 2
    return x


def _block_start(axis, size, rows):
    idx = lax.axis_index(axis)
    start = 0
    d, span = 1, rows
    while 2 * d < size:
        span //= 2
        start = start + ((idx // d) % 2) * span
        d *= 2
    return start


def _pick(x, axis, take_low):
    n = x.shape[axis] // 2
    lo = lax.slice_in_dim(x, 0, n, axis=axis)
    hi = lax.slice_in_dim(x, n, 2 * n, axis=axis)
    return jnp.where(take_low, lo, hi)


def _rows_back(a, w, rf_own, rf_for_partner, col_factor):
    scaled = (a.astype(jnp.float32) * w.astype(jnp.float32)[None]).astype(jnp.bfloat16)
    projected = jnp.einsum(
        "mrn,nc->mrc", scaled, col_factor, preferred_element_type=jnp.float32
    ).astype(jnp.bfloat16)
    n_m = projected.shape[0]
    mh = n_m // 2
    chunks = [(0, mh), (mh, n_m)] if mh > 0 else [(0, n_m)]
    summed = jnp.einsum("rk,mrc->kmc", rf_own, projected, preferred_element_type=jnp.float32)
    other = []
    for lo, hi in chunks:
        proj_other = _swap(projected[lo:hi], "half")
        other.append(jnp.einsum(
            "rk,mrc->kmc", rf_for_partner, proj_other, preferred_element_type=jnp.float32
        ))
    return summed + jnp.concatenate(other, axis=1)


def local(anomalies, control, precision, row_factor, col_factor, n_mem):
    h = lax.axis_index("half")
    kh = control.shape[0]
    rows = anomalies.shape[0]
    n_lev = anomalies.shape[2]

    anom_t = jnp.transpose(anomalies, (2, 1, 0, 3))
    prec_t = jnp.transpose(precision, (1, 0, 2))

    rf_own = lax.dynamic_slice_in_dim(row_factor, h * kh, kh, 1)
    rf_other = lax.dynamic_slice_in_dim(row_factor, (1 - h) * kh, kh, 1)
    rf_for_partner = _swap(rf_other, "half")
    ctrl_other = _swap(control, "half")
    expanded_all = (
        jnp.einsum("rk,kmlc->lmrc", rf_own, control, preferred_element_type=jnp.float32)
        + jnp.einsum("rk,kmlc->lmrc", rf_other, ctrl_other, preferred_element_type=jnp.float32)
    ).astype(jnp.bfloat16)

    pow2 = n_mem & (n_mem - 1) == 0 and rows % n_mem == 0
    blk = rows // max(n_mem // 2, 1)
    start = _block_start("mem", n_mem, rows) if pow2 else 0

    outs = []
    for l in range(n_lev):
        a = anom_t[l]
        expanded = expanded_all[l]
        fields = jnp.einsum("mrc,nc->mrn", expanded, col_factor, preferred_element_type=jnp.float32)
        inc = jnp.sum(a.astype(jnp.float32) * fields, axis=0)
        prec = prec_t[l]
        if pow2 and n_mem == 4:
            part = _reduce_scatter_rows(inc, "mem", n_mem, jnp.bfloat16)
            w_blk = (lax.dynamic_slice_in_dim(prec, start, blk, 0) * part).astype(jnp.bfloat16)
            w_recv = lax.ppermute(w_blk, "mem", [(i, i ^ 1) for i in range(n_mem)])
            low_first = lax.axis_index("mem") % 2 == 0
            summed = None
            for w, own in ((w_blk, True), (w_recv, False)):
                take_low = low_first if own else jnp.logical_not(low_first)
                part_sum = _rows_back(
                    _pick(a, 1, take_low), w, _pick(rf_own, 0, take_low),
                    _pick(rf_for_partner, 0, take_low), col_factor,
                )
                summed = part_sum if summed is None else summed + part_sum
        else:
            if pow2:
                part = _reduce_scatter_rows(inc, "mem", n_mem, jnp.bfloat16)
                w_blk = (lax.dynamic_slice_in_dim(prec, start, blk, 0) * part).astype(jnp.bfloat16)
                weighted = _all_gather_rows(w_blk, "mem", n_mem)
            else:
                weighted = (prec * lax.psum(inc, "mem")).astype(jnp.bfloat16)
            summed = _rows_back(a, weighted, rf_own, rf_for_partner, col_factor)
        outs.append(summed)
    return (control.astype(jnp.float32) + jnp.stack(outs, axis=2)).astype(jnp.bfloat16)


def solution(mesh):
    n_mem = mesh.shape["mem"]

    def f(anomalies, control, precision, row_factor, col_factor):
        return local(anomalies, control, precision, row_factor, col_factor, n_mem)

    return jax.shard_map(
        f,
        mesh=mesh,
        in_specs=(
            P("half", ("grp", "mem"), "lev", None),
            P("half", ("grp", "mem"), "lev", None),
            P("half", ("grp", "lev"), None),
            P("half", None),
            P(),
        ),
        out_specs=P("half", ("grp", "mem"), "lev", None),
        check_vma=False,
    )
```

```python
import jax
import jax.numpy as jnp
from jax import lax
from jax.sharding import PartitionSpec as P


def _swap(x, axis):
    return lax.ppermute(x, axis, [(0, 1), (1, 0)])


def _reduce_scatter_rows(x, axis, size, wire):
    idx = lax.axis_index(axis)
    d = 1
    while 2 * d < size:
        half = x.shape[0] // 2
        bit = (idx // d) % 2
        keep = lax.dynamic_slice_in_dim(x, bit * half, half, 0)
        send = lax.dynamic_slice_in_dim(x, (1 - bit) * half, half, 0)
        recv = lax.ppermute(send.astype(wire), axis, [(i, i ^ d) for i in range(size)])
        x = keep + recv.astype(x.dtype)
        d *= 2
    if d < size:
        recv = lax.ppermute(x.astype(wire), axis, [(i, i ^ d) for i in range(size)])
        x = x + recv.astype(x.dtype)
    return x


def _all_gather_rows(x, axis, size):
    idx = lax.axis_index(axis)
    d = size // 4
    while d >= 1:
        bit = (idx // d) % 2
        recv = lax.ppermute(x, axis, [(i, i ^ d) for i in range(size)])
        lo = jnp.where(bit == 0, x, recv)
        hi = jnp.where(bit == 0, recv, x)
        x = jnp.concatenate([lo, hi], axis=0)
        d //= 2
    return x


def _block_start(axis, size, rows):
    idx = lax.axis_index(axis)
    start = 0
    d, span = 1, rows
    while 2 * d < size:
        span //= 2
        start = start + ((idx // d) % 2) * span
        d *= 2
    return start


def local(anomalies, control, precision, row_factor, col_factor, n_mem):
    h = lax.axis_index("half")
    kh = control.shape[0]
    rows = anomalies.shape[0]
    n_lev = anomalies.shape[2]

    anom_t = jnp.transpose(anomalies, (2, 1, 0, 3))

    rf_own = lax.dynamic_slice_in_dim(row_factor, h * kh, kh, 1)
    rf_other = lax.dynamic_slice_in_dim(row_factor, (1 - h) * kh, kh, 1)
    rf_for_partner = _swap(rf_other, "half")
    ctrl_other = _swap(control, "half")
    expanded_all = (
        jnp.einsum("rk,kmlc->lmrc", rf_own, control, preferred_element_type=jnp.float32)
        + jnp.einsum("rk,kmlc->lmrc", rf_other, ctrl_other, preferred_element_type=jnp.float32)
    ).astype(jnp.bfloat16)

    pow2 = n_mem & (n_mem - 1) == 0 and rows % n_mem == 0
    blk = rows // max(n_mem // 2, 1)
    start = _block_start("mem", n_mem, rows) if pow2 else 0

    outs = []
    for l in range(n_lev):
        a = anom_t[l]
        expanded = expanded_all[l]
        fields = jnp.einsum("mrc,nc->mrn", expanded, col_factor, preferred_element_type=jnp.float32)
        inc = jnp.sum(a.astype(jnp.float32) * fields, axis=0)
        if pow2:
            part = _reduce_scatter_rows(inc, "mem", n_mem, jnp.bfloat16)
            prec_blk = lax.dynamic_slice(precision, (start, l, 0), (blk, 1, precision.shape[2]))
            w_blk = (prec_blk[:, 0, :] * part).astype(jnp.bfloat16)
            weighted = _all_gather_rows(w_blk, "mem", n_mem)
        else:
            weighted = (precision[:, l, :] * lax.psum(inc, "mem")).astype(jnp.bfloat16)
        scaled = (a.astype(jnp.float32) * weighted.astype(jnp.float32)[None]).astype(jnp.bfloat16)
        projected = jnp.einsum(
            "mrn,nc->mrc", scaled, col_factor, preferred_element_type=jnp.float32
        ).astype(jnp.bfloat16)
        n_m = projected.shape[0]
        mh = n_m // 2
        chunks = [(0, mh), (mh, n_m)] if mh > 0 else [(0, n_m)]
        summed = jnp.einsum("rk,mrc->kmc", rf_own, projected, preferred_element_type=jnp.float32)
        other = []
        for lo, hi in chunks:
            proj_other = _swap(projected[lo:hi], "half")
            other.append(jnp.einsum(
                "rk,mrc->kmc", rf_for_partner, proj_other, preferred_element_type=jnp.float32
            ))
        summed = summed + jnp.concatenate(other, axis=1)
        outs.append(summed)
    return (control.astype(jnp.float32) + jnp.stack(outs, axis=2)).astype(jnp.bfloat16)


def solution(mesh):
    n_mem = mesh.shape["mem"]

    def f(anomalies, control, precision, row_factor, col_factor):
        return local(anomalies, control, precision, row_factor, col_factor, n_mem)

    return jax.shard_map(
        f,
        mesh=mesh,
        in_specs=(
            P("half", ("grp", "mem"), "lev", None),
            P("half", ("grp", "mem"), "lev", None),
            P("half", ("grp", "lev"), None),
            P("half", None),
            P(),
        ),
        out_specs=P("half", ("grp", "mem"), "lev", None),
        check_vma=False,
    )
```

```python
import jax
import jax.numpy as jnp
from jax import lax
from jax.sharding import PartitionSpec as P


def _swap(x, axis):
    return lax.ppermute(x, axis, [(0, 1), (1, 0)])


def _reduce_scatter_rows(x, axis, size, wire):
    idx = lax.axis_index(axis)
    d = 1
    while 2 * d < size:
        half = x.shape[0] // 2
        bit = (idx // d) % 2
        keep = lax.dynamic_slice_in_dim(x, bit * half, half, 0)
        send = lax.dynamic_slice_in_dim(x, (1 - bit) * half, half, 0)
        recv = lax.ppermute(send.astype(wire), axis, [(i, i ^ d) for i in range(size)])
        x = keep + recv.astype(x.dtype)
        d *= 2
    if d < size:
        recv = lax.ppermute(x.astype(wire), axis, [(i, i ^ d) for i in range(size)])
        x = x + recv.astype(x.dtype)
    return x


def _all_gather_rows(x, axis, size):
    idx = lax.axis_index(axis)
    d = size // 4
    while d >= 1:
        bit = (idx // d) % 2
        recv = lax.ppermute(x, axis, [(i, i ^ d) for i in range(size)])
        lo = jnp.where(bit == 0, x, recv)
        hi = jnp.where(bit == 0, recv, x)
        x = jnp.concatenate([lo, hi], axis=0)
        d //= 2
    return x


def _block_start(axis, size, rows):
    idx = lax.axis_index(axis)
    start = 0
    d, span = 1, rows
    while 2 * d < size:
        span //= 2
        start = start + ((idx // d) % 2) * span
        d *= 2
    return start


def local(anomalies, control, precision, row_factor, col_factor, n_mem):
    h = lax.axis_index("half")
    kh = control.shape[0]
    rows = anomalies.shape[0]
    n_lev = anomalies.shape[2]

    anom_t = jnp.transpose(anomalies, (2, 1, 0, 3))

    rf_own = lax.dynamic_slice_in_dim(row_factor, h * kh, kh, 1)
    rf_other = lax.dynamic_slice_in_dim(row_factor, (1 - h) * kh, kh, 1)
    rf_for_partner = _swap(rf_other, "half")
    ctrl_other = _swap(control, "half")
    expanded_all = (
        jnp.einsum("rk,kmlc->lmrc", rf_own, control, preferred_element_type=jnp.float32)
        + jnp.einsum("rk,kmlc->lmrc", rf_other, ctrl_other, preferred_element_type=jnp.float32)
    ).astype(jnp.bfloat16)

    pow2 = n_mem & (n_mem - 1) == 0 and rows % n_mem == 0
    blk = rows // max(n_mem // 2, 1)
    start = _block_start("mem", n_mem, rows) if pow2 else 0

    outs = []
    for l in range(n_lev):
        a = anom_t[l]
        expanded = expanded_all[l]
        fields = jnp.einsum("mrc,nc->mrn", expanded, col_factor, preferred_element_type=jnp.float32)
        inc = jnp.sum(a.astype(jnp.float32) * fields, axis=0)
        if l == 0:
            precision, inc = lax.optimization_barrier((precision, inc))
            prec_t = jnp.transpose(precision, (1, 0, 2))
        prec = prec_t[l]
        if pow2:
            part = _reduce_scatter_rows(inc, "mem", n_mem, jnp.bfloat16)
            w_blk = (lax.dynamic_slice_in_dim(prec, start, blk, 0) * part).astype(jnp.bfloat16)
            weighted = _all_gather_rows(w_blk, "mem", n_mem)
        else:
            weighted = (prec * lax.psum(inc, "mem")).astype(jnp.bfloat16)
        scaled = (a.astype(jnp.float32) * weighted.astype(jnp.float32)[None]).astype(jnp.bfloat16)
        projected = jnp.einsum(
            "mrn,nc->mrc", scaled, col_factor, preferred_element_type=jnp.float32
        ).astype(jnp.bfloat16)
        n_m = projected.shape[0]
        cuts = [i * n_m // 3 for i in range(4)]
        chunks = [(lo, hi) for lo, hi in zip(cuts[:-1], cuts[1:]) if lo < hi]
        summed = jnp.einsum("rk,mrc->kmc", rf_own, projected, preferred_element_type=jnp.float32)
        other = []
        for lo, hi in chunks:
            proj_other = _swap(projected[lo:hi], "half")
            other.append(jnp.einsum(
                "rk,mrc->kmc", rf_for_partner, proj_other, preferred_element_type=jnp.float32
            ))
        summed = summed + jnp.concatenate(other, axis=1)
        outs.append(summed)
    return (control.astype(jnp.float32) + jnp.stack(outs, axis=2)).astype(jnp.bfloat16)


def solution(mesh):
    n_mem = mesh.shape["mem"]

    def f(anomalies, control, precision, row_factor, col_factor):
        return local(anomalies, control, precision, row_factor, col_factor, n_mem)

    return jax.shard_map(
        f,
        mesh=mesh,
        in_specs=(
            P("half", ("grp", "mem"), "lev", None),
            P("half", ("grp", "mem"), "lev", None),
            P("half", ("grp", "lev"), None),
            P("half", None),
            P(),
        ),
        out_specs=P("half", ("grp", "mem"), "lev", None),
        check_vma=False,
    )
```

```python
import jax
import jax.numpy as jnp
from jax import lax
from jax.sharding import PartitionSpec as P


def _swap(x, axis):
    return lax.ppermute(x, axis, [(0, 1), (1, 0)])


def _reduce_scatter_rows(x, axis, size, wire, hold):
    idx = lax.axis_index(axis)
    d = 1
    first = True
    while 2 * d < size:
        half = x.shape[0] // 2
        bit = (idx // d) % 2
        keep = lax.dynamic_slice_in_dim(x, bit * half, half, 0)
        send = lax.dynamic_slice_in_dim(x, (1 - bit) * half, half, 0).astype(wire)
        if first:
            send, hold = lax.optimization_barrier((send, hold))
            first = False
        recv = lax.ppermute(send, axis, [(i, i ^ d) for i in range(size)])
        x = keep + recv.astype(x.dtype)
        d *= 2
    if d < size:
        send = x.astype(wire)
        if first:
            send, hold = lax.optimization_barrier((send, hold))
        recv = lax.ppermute(send, axis, [(i, i ^ d) for i in range(size)])
        x = x + recv.astype(x.dtype)
    return x, hold


def _all_gather_rows(x, axis, size):
    idx = lax.axis_index(axis)
    d = size // 4
    while d >= 1:
        bit = (idx // d) % 2
        recv = lax.ppermute(x, axis, [(i, i ^ d) for i in range(size)])
        lo = jnp.where(bit == 0, x, recv)
        hi = jnp.where(bit == 0, recv, x)
        x = jnp.concatenate([lo, hi], axis=0)
        d //= 2
    return x


def _block_start(axis, size, rows):
    idx = lax.axis_index(axis)
    start = 0
    d, span = 1, rows
    while 2 * d < size:
        span //= 2
        start = start + ((idx // d) % 2) * span
        d *= 2
    return start


def local(anomalies, control, precision, row_factor, col_factor, n_mem):
    h = lax.axis_index("half")
    kh = control.shape[0]
    rows = anomalies.shape[0]
    n_lev = anomalies.shape[2]

    anom_t = jnp.transpose(anomalies, (2, 1, 0, 3))

    rf_own = lax.dynamic_slice_in_dim(row_factor, h * kh, kh, 1)
    rf_other = lax.dynamic_slice_in_dim(row_factor, (1 - h) * kh, kh, 1)
    rf_for_partner = _swap(rf_other, "half")
    ctrl_other = _swap(control, "half")
    expanded_all = (
        jnp.einsum("rk,kmlc->lmrc", rf_own, control, preferred_element_type=jnp.float32)
        + jnp.einsum("rk,kmlc->lmrc", rf_other, ctrl_other, preferred_element_type=jnp.float32)
    ).astype(jnp.bfloat16)

    pow2 = n_mem & (n_mem - 1) == 0 and rows % n_mem == 0
    blk = rows // max(n_mem // 2, 1)
    start = _block_start("mem", n_mem, rows) if pow2 else 0

    outs = []
    cf_next = col_factor
    for l in range(n_lev):
        a = anom_t[l]
        expanded = expanded_all[l]
        fields = jnp.einsum("mrc,nc->mrn", expanded, cf_next, preferred_element_type=jnp.float32)
        inc = jnp.sum(a.astype(jnp.float32) * fields, axis=0)
        if l == 0:
            precision, inc = lax.optimization_barrier((precision, inc))
            prec_t = jnp.transpose(precision, (1, 0, 2))
        prec = prec_t[l]
        if pow2:
            part, cf_next = _reduce_scatter_rows(inc, "mem", n_mem, jnp.bfloat16, col_factor)
            w_blk = (lax.dynamic_slice_in_dim(prec, start, blk, 0) * part).astype(jnp.bfloat16)
            weighted = _all_gather_rows(w_blk, "mem", n_mem)
        else:
            weighted = (prec * lax.psum(inc, "mem")).astype(jnp.bfloat16)
        scaled = (a.astype(jnp.float32) * weighted.astype(jnp.float32)[None]).astype(jnp.bfloat16)
        projected = jnp.einsum(
            "mrn,nc->mrc", scaled, col_factor, preferred_element_type=jnp.float32
        ).astype(jnp.bfloat16)
        n_m = projected.shape[0]
        cuts = [i * n_m // 3 for i in range(4)]
        chunks = [(lo, hi) for lo, hi in zip(cuts[:-1], cuts[1:]) if lo < hi]
        summed = jnp.einsum("rk,mrc->kmc", rf_own, projected, preferred_element_type=jnp.float32)
        other = []
        for lo, hi in chunks:
            proj_other = _swap(projected[lo:hi], "half")
            other.append(jnp.einsum(
                "rk,mrc->kmc", rf_for_partner, proj_other, preferred_element_type=jnp.float32
            ))
        summed = summed + jnp.concatenate(other, axis=1)
        outs.append(summed)
    return (control.astype(jnp.float32) + jnp.stack(outs, axis=2)).astype(jnp.bfloat16)


def solution(mesh):
    n_mem = mesh.shape["mem"]

    def f(anomalies, control, precision, row_factor, col_factor):
        return local(anomalies, control, precision, row_factor, col_factor, n_mem)

    return jax.shard_map(
        f,
        mesh=mesh,
        in_specs=(
            P("half", ("grp", "mem"), "lev", None),
            P("half", ("grp", "mem"), "lev", None),
            P("half", ("grp", "lev"), None),
            P("half", None),
            P(),
        ),
        out_specs=P("half", ("grp", "mem"), "lev", None),
        check_vma=False,
    )
```

```python
import jax
import jax.numpy as jnp
from jax import lax
from jax.sharding import PartitionSpec as P


def _swap(x, axis):
    return lax.ppermute(x, axis, [(0, 1), (1, 0)])


def _reduce_scatter_rows(x, axis, size, wire, hold):
    idx = lax.axis_index(axis)
    d = 1
    first = True
    while 2 * d < size:
        half = x.shape[0] // 2
        bit = (idx // d) % 2
        keep = lax.dynamic_slice_in_dim(x, bit * half, half, 0)
        send = lax.dynamic_slice_in_dim(x, (1 - bit) * half, half, 0).astype(wire)
        if first:
            send, hold = lax.optimization_barrier((send, hold))
            first = False
        recv = lax.ppermute(send, axis, [(i, i ^ d) for i in range(size)])
        x = keep + recv.astype(x.dtype)
        d *= 2
    if d < size:
        send = x.astype(wire)
        if first:
            send, hold = lax.optimization_barrier((send, hold))
        recv = lax.ppermute(send, axis, [(i, i ^ d) for i in range(size)])
        x = x + recv.astype(x.dtype)
    return x, hold


def _all_gather_rows(x, axis, size):
    idx = lax.axis_index(axis)
    d = size // 4
    while d >= 1:
        bit = (idx // d) % 2
        recv = lax.ppermute(x, axis, [(i, i ^ d) for i in range(size)])
        lo = jnp.where(bit == 0, x, recv)
        hi = jnp.where(bit == 0, recv, x)
        x = jnp.concatenate([lo, hi], axis=0)
        d //= 2
    return x


def _block_start(axis, size, rows):
    idx = lax.axis_index(axis)
    start = 0
    d, span = 1, rows
    while 2 * d < size:
        span //= 2
        start = start + ((idx // d) % 2) * span
        d *= 2
    return start


def local(anomalies, control, precision, row_factor, col_factor, n_mem):
    h = lax.axis_index("half")
    kh = control.shape[0]
    rows = anomalies.shape[0]
    n_lev = anomalies.shape[2]

    anom_t = jnp.transpose(anomalies, (2, 1, 0, 3))

    rf_own = lax.dynamic_slice_in_dim(row_factor, h * kh, kh, 1)
    rf_other = lax.dynamic_slice_in_dim(row_factor, (1 - h) * kh, kh, 1)
    ctrl_other = _swap(control, "half")
    expanded_all = (
        jnp.einsum("rk,kmlc->lmrc", rf_own, control, preferred_element_type=jnp.float32)
        + jnp.einsum("rk,kmlc->lmrc", rf_other, ctrl_other, preferred_element_type=jnp.float32)
    ).astype(jnp.bfloat16)

    pow2 = n_mem & (n_mem - 1) == 0 and rows % n_mem == 0
    blk = rows // max(n_mem // 2, 1)
    start = _block_start("mem", n_mem, rows) if pow2 else 0

    outs = []
    cf_next = col_factor
    rf_send = row_factor
    for l in range(n_lev):
        a = anom_t[l]
        expanded = expanded_all[l]
        fields = jnp.einsum("mrc,nc->mrn", expanded, cf_next, preferred_element_type=jnp.float32)
        inc = jnp.sum(a.astype(jnp.float32) * fields, axis=0)
        if l == 0:
            precision, inc = lax.optimization_barrier((precision, inc))
            prec_t = jnp.transpose(precision, (1, 0, 2))
        prec = prec_t[l]
        if pow2:
            part, (cf_next, rf_send) = _reduce_scatter_rows(
                inc, "mem", n_mem, jnp.bfloat16, (col_factor, rf_send))
            w_blk = (lax.dynamic_slice_in_dim(prec, start, blk, 0) * part).astype(jnp.bfloat16)
            weighted = _all_gather_rows(w_blk, "mem", n_mem)
        else:
            weighted = (prec * lax.psum(inc, "mem")).astype(jnp.bfloat16)
        if l == 0:
            rf_for_partner = _swap(lax.dynamic_slice_in_dim(rf_send, (1 - h) * kh, kh, 1), "half")
        scaled = (a.astype(jnp.float32) * weighted.astype(jnp.float32)[None]).astype(jnp.bfloat16)
        projected = jnp.einsum(
            "mrn,nc->mrc", scaled, col_factor, preferred_element_type=jnp.float32
        ).astype(jnp.bfloat16)
        n_m = projected.shape[0]
        cuts = [i * n_m // 3 for i in range(4)]
        chunks = [(lo, hi) for lo, hi in zip(cuts[:-1], cuts[1:]) if lo < hi]
        summed = jnp.einsum("rk,mrc->kmc", rf_own, projected, preferred_element_type=jnp.float32)
        other = []
        for lo, hi in chunks:
            proj_other = _swap(projected[lo:hi], "half")
            other.append(jnp.einsum(
                "rk,mrc->kmc", rf_for_partner, proj_other, preferred_element_type=jnp.float32
            ))
        summed = summed + jnp.concatenate(other, axis=1)
        outs.append(summed)
    return (control.astype(jnp.float32) + jnp.stack(outs, axis=2)).astype(jnp.bfloat16)


def solution(mesh):
    n_mem = mesh.shape["mem"]

    def f(anomalies, control, precision, row_factor, col_factor):
        return local(anomalies, control, precision, row_factor, col_factor, n_mem)

    return jax.shard_map(
        f,
        mesh=mesh,
        in_specs=(
            P("half", ("grp", "mem"), "lev", None),
            P("half", ("grp", "mem"), "lev", None),
            P("half", ("grp", "lev"), None),
            P("half", None),
            P(),
        ),
        out_specs=P("half", ("grp", "mem"), "lev", None),
        check_vma=False,
    )
```

```python
import jax
import jax.numpy as jnp
from jax import lax
from jax.sharding import PartitionSpec as P


def _swap(x, axis):
    return lax.ppermute(x, axis, [(0, 1), (1, 0)])


def _reduce_scatter_rows(x, axis, size, wire, hold):
    idx = lax.axis_index(axis)
    d = 1
    first = True
    while 2 * d < size:
        half = x.shape[0] // 2
        bit = (idx // d) % 2
        keep = lax.dynamic_slice_in_dim(x, bit * half, half, 0)
        send = lax.dynamic_slice_in_dim(x, (1 - bit) * half, half, 0).astype(wire)
        if first:
            send, hold = lax.optimization_barrier((send, hold))
            first = False
        recv = lax.ppermute(send, axis, [(i, i ^ d) for i in range(size)])
        x = keep + recv.astype(x.dtype)
        d *= 2
    if d < size:
        send = x.astype(wire)
        if first:
            send, hold = lax.optimization_barrier((send, hold))
        recv = lax.ppermute(send, axis, [(i, i ^ d) for i in range(size)])
        x = x + recv.astype(x.dtype)
    return x, hold


def _all_gather_rows(x, axis, size):
    idx = lax.axis_index(axis)
    d = size // 4
    while d >= 1:
        bit = (idx // d) % 2
        recv = lax.ppermute(x, axis, [(i, i ^ d) for i in range(size)])
        lo = jnp.where(bit == 0, x, recv)
        hi = jnp.where(bit == 0, recv, x)
        x = jnp.concatenate([lo, hi], axis=0)
        d //= 2
    return x


def _block_start(axis, size, rows):
    idx = lax.axis_index(axis)
    start = 0
    d, span = 1, rows
    while 2 * d < size:
        span //= 2
        start = start + ((idx // d) % 2) * span
        d *= 2
    return start


def local(anomalies, control, precision, row_factor, col_factor, n_mem):
    h = lax.axis_index("half")
    kh = control.shape[0]
    rows = anomalies.shape[0]
    n_lev = anomalies.shape[2]

    anom_t = jnp.transpose(anomalies, (2, 1, 0, 3))

    rf_own = lax.dynamic_slice_in_dim(row_factor, h * kh, kh, 1)
    rf_other = lax.dynamic_slice_in_dim(row_factor, (1 - h) * kh, kh, 1)
    rf_for_partner = _swap(rf_other, "half")
    ctrl_other = _swap(control, "half")
    expanded_all = (
        jnp.einsum("rk,kmlc->lmrc", rf_own, control, preferred_element_type=jnp.float32)
        + jnp.einsum("rk,kmlc->lmrc", rf_other, ctrl_other, preferred_element_type=jnp.float32)
    ).astype(jnp.bfloat16)

    pow2 = n_mem & (n_mem - 1) == 0 and rows % n_mem == 0
    blk = rows // max(n_mem // 2, 1)
    start = _block_start("mem", n_mem, rows) if pow2 else 0

    outs = []
    cf_next = col_factor
    parts = []
    for l in range(n_lev):
        a = anom_t[l]
        expanded = expanded_all[l]
        fields = jnp.einsum("mrc,nc->mrn", expanded, cf_next, preferred_element_type=jnp.float32)
        inc = jnp.sum(a.astype(jnp.float32) * fields, axis=0)
        if pow2:
            if l + 1 < n_lev:
                part, cf_next = _reduce_scatter_rows(inc, "mem", n_mem, jnp.bfloat16, col_factor)
            else:
                part, precision = _reduce_scatter_rows(inc, "mem", n_mem, jnp.bfloat16, precision)
        else:
            part = inc
        parts.append(part)
    prec_t = jnp.transpose(precision, (1, 0, 2))
    for l in range(n_lev):
        a = anom_t[l]
        part = parts[l]
        prec = prec_t[l]
        if pow2:
            w_blk = (lax.dynamic_slice_in_dim(prec, start, blk, 0) * part).astype(jnp.bfloat16)
            weighted = _all_gather_rows(w_blk, "mem", n_mem)
        else:
            weighted = (prec * lax.psum(part, "mem")).astype(jnp.bfloat16)
        scaled = (a.astype(jnp.float32) * weighted.astype(jnp.float32)[None]).astype(jnp.bfloat16)
        projected = jnp.einsum(
            "mrn,nc->mrc", scaled, col_factor, preferred_element_type=jnp.float32
        ).astype(jnp.bfloat16)
        n_m = projected.shape[0]
        cuts = [i * n_m // 3 for i in range(4)]
        chunks = [(lo, hi) for lo, hi in zip(cuts[:-1], cuts[1:]) if lo < hi]
        summed = jnp.einsum("rk,mrc->kmc", rf_own, projected, preferred_element_type=jnp.float32)
        other = []
        for lo, hi in chunks:
            proj_other = _swap(projected[lo:hi], "half")
            other.append(jnp.einsum(
                "rk,mrc->kmc", rf_for_partner, proj_other, preferred_element_type=jnp.float32
            ))
        summed = summed + jnp.concatenate(other, axis=1)
        outs.append(summed)
    return (control.astype(jnp.float32) + jnp.stack(outs, axis=2)).astype(jnp.bfloat16)


def solution(mesh):
    n_mem = mesh.shape["mem"]

    def f(anomalies, control, precision, row_factor, col_factor):
        return local(anomalies, control, precision, row_factor, col_factor, n_mem)

    return jax.shard_map(
        f,
        mesh=mesh,
        in_specs=(
            P("half", ("grp", "mem"), "lev", None),
            P("half", ("grp", "mem"), "lev", None),
            P("half", ("grp", "lev"), None),
            P("half", None),
            P(),
        ),
        out_specs=P("half", ("grp", "mem"), "lev", None),
        check_vma=False,
    )
```

```python
import jax
import jax.numpy as jnp
from jax import lax
from jax.sharding import PartitionSpec as P


def _swap(x, axis):
    return lax.ppermute(x, axis, [(0, 1), (1, 0)])


def _reduce_scatter_rows(x, axis, size, wire, hold):
    idx = lax.axis_index(axis)
    d = 1
    first = True
    while 2 * d < size:
        half = x.shape[0] // 2
        bit = (idx // d) % 2
        keep = lax.dynamic_slice_in_dim(x, bit * half, half, 0)
        send = lax.dynamic_slice_in_dim(x, (1 - bit) * half, half, 0).astype(wire)
        if first:
            send, hold = lax.optimization_barrier((send, hold))
            first = False
        recv = lax.ppermute(send, axis, [(i, i ^ d) for i in range(size)])
        x = keep + recv.astype(x.dtype)
        d *= 2
    if d < size:
        send = x.astype(wire)
        if first:
            send, hold = lax.optimization_barrier((send, hold))
        recv = lax.ppermute(send, axis, [(i, i ^ d) for i in range(size)])
        x = x + recv.astype(x.dtype)
    return x, hold


def _all_gather_rows(x, axis, size):
    idx = lax.axis_index(axis)
    d = size // 4
    while d >= 1:
        bit = (idx // d) % 2
        recv = lax.ppermute(x, axis, [(i, i ^ d) for i in range(size)])
        lo = jnp.where(bit == 0, x, recv)
        hi = jnp.where(bit == 0, recv, x)
        x = jnp.concatenate([lo, hi], axis=0)
        d //= 2
    return x


def _block_start(axis, size, rows):
    idx = lax.axis_index(axis)
    start = 0
    d, span = 1, rows
    while 2 * d < size:
        span //= 2
        start = start + ((idx // d) % 2) * span
        d *= 2
    return start


def local(anomalies, control, precision, row_factor, col_factor, n_mem):
    h = lax.axis_index("half")
    kh = control.shape[0]
    rows = anomalies.shape[0]
    n_lev = anomalies.shape[2]

    anom_t = jnp.transpose(anomalies, (2, 1, 0, 3))

    rf_own = lax.dynamic_slice_in_dim(row_factor, h * kh, kh, 1)
    rf_other = lax.dynamic_slice_in_dim(row_factor, (1 - h) * kh, kh, 1)
    ctrl_other = _swap(control, "half")
    expanded_all = (
        jnp.einsum("rk,kmlc->lmrc", rf_own, control, preferred_element_type=jnp.float32)
        + jnp.einsum("rk,kmlc->lmrc", rf_other, ctrl_other, preferred_element_type=jnp.float32)
    ).astype(jnp.bfloat16)

    pow2 = n_mem & (n_mem - 1) == 0 and rows % n_mem == 0
    blk = rows // max(n_mem // 2, 1)
    start = _block_start("mem", n_mem, rows) if pow2 else 0

    outs = []
    cf_next = col_factor
    for l in range(n_lev):
        a = anom_t[l]
        expanded = expanded_all[l]
        fields = jnp.einsum("mrc,nc->mrn", expanded, cf_next, preferred_element_type=jnp.float32)
        inc = jnp.sum(a.astype(jnp.float32) * fields, axis=0)
        if l == 0:
            precision, inc = lax.optimization_barrier((precision, inc))
            prec_t = jnp.transpose(precision, (1, 0, 2))
        prec = prec_t[l]
        if pow2:
            part, cf_next = _reduce_scatter_rows(inc, "mem", n_mem, jnp.bfloat16, col_factor)
            w_blk = (lax.dynamic_slice_in_dim(prec, start, blk, 0) * part).astype(jnp.bfloat16)
            weighted = _all_gather_rows(w_blk, "mem", n_mem)
        else:
            weighted = (prec * lax.psum(inc, "mem")).astype(jnp.bfloat16)
        scaled = (a.astype(jnp.float32) * weighted.astype(jnp.float32)[None]).astype(jnp.bfloat16)
        projected = jnp.einsum(
            "mrn,nc->mrc", scaled, col_factor, preferred_element_type=jnp.float32
        ).astype(jnp.bfloat16)
        n_m = projected.shape[0]
        cuts = [i * n_m // 3 for i in range(4)]
        chunks = [(lo, hi) for lo, hi in zip(cuts[:-1], cuts[1:]) if lo < hi]
        summed = jnp.einsum("rk,mrc->kmc", rf_own, projected, preferred_element_type=jnp.float32)
        other = []
        for lo, hi in chunks:
            for_partner = jnp.einsum(
                "rk,mrc->kmc", rf_other, projected[lo:hi], preferred_element_type=jnp.float32
            )
            other.append(_swap(for_partner, "half"))
        summed = summed + jnp.concatenate(other, axis=1)
        outs.append(summed)
    return (control.astype(jnp.float32) + jnp.stack(outs, axis=2)).astype(jnp.bfloat16)


def solution(mesh):
    n_mem = mesh.shape["mem"]

    def f(anomalies, control, precision, row_factor, col_factor):
        return local(anomalies, control, precision, row_factor, col_factor, n_mem)

    return jax.shard_map(
        f,
        mesh=mesh,
        in_specs=(
            P("half", ("grp", "mem"), "lev", None),
            P("half", ("grp", "mem"), "lev", None),
            P("half", ("grp", "lev"), None),
            P("half", None),
            P(),
        ),
        out_specs=P("half", ("grp", "mem"), "lev", None),
        check_vma=False,
    )
```

```python
import jax
import jax.numpy as jnp
from jax import lax
from jax.sharding import PartitionSpec as P


def _swap(x, axis):
    return lax.ppermute(x, axis, [(0, 1), (1, 0)])


def _reduce_scatter_rows(x, axis, size, wire, hold):
    idx = lax.axis_index(axis)
    d = 1
    first = True
    while 2 * d < size:
        half = x.shape[0] // 2
        bit = (idx // d) % 2
        keep = lax.dynamic_slice_in_dim(x, bit * half, half, 0)
        send = lax.dynamic_slice_in_dim(x, (1 - bit) * half, half, 0).astype(wire)
        if first:
            send, hold = lax.optimization_barrier((send, hold))
            first = False
        recv = lax.ppermute(send, axis, [(i, i ^ d) for i in range(size)])
        x = keep + recv.astype(x.dtype)
        d *= 2
    if d < size:
        send = x.astype(wire)
        if first:
            send, hold = lax.optimization_barrier((send, hold))
        recv = lax.ppermute(send, axis, [(i, i ^ d) for i in range(size)])
        x = x + recv.astype(x.dtype)
    return x, hold


def _all_gather_rows(x, axis, size):
    idx = lax.axis_index(axis)
    d = size // 4
    while d >= 1:
        bit = (idx // d) % 2
        recv = lax.ppermute(x, axis, [(i, i ^ d) for i in range(size)])
        lo = jnp.where(bit == 0, x, recv)
        hi = jnp.where(bit == 0, recv, x)
        x = jnp.concatenate([lo, hi], axis=0)
        d //= 2
    return x


def _block_start(axis, size, rows):
    idx = lax.axis_index(axis)
    start = 0
    d, span = 1, rows
    while 2 * d < size:
        span //= 2
        start = start + ((idx // d) % 2) * span
        d *= 2
    return start


def local(anomalies, control, precision, row_factor, col_factor, n_mem):
    h = lax.axis_index("half")
    kh = control.shape[0]
    rows = anomalies.shape[0]
    n_lev = anomalies.shape[2]

    anom_t = jnp.transpose(anomalies, (2, 1, 0, 3))

    rf_own = lax.dynamic_slice_in_dim(row_factor, h * kh, kh, 1)
    rf_other = lax.dynamic_slice_in_dim(row_factor, (1 - h) * kh, kh, 1)
    rf_partner = _swap(row_factor, "half")
    ctrl_other = _swap(control, "half")
    expanded_all = (
        jnp.einsum("rk,kmlc->lmrc", rf_own, control, preferred_element_type=jnp.float32)
        + jnp.einsum("rk,kmlc->lmrc", rf_other, ctrl_other, preferred_element_type=jnp.float32)
    ).astype(jnp.bfloat16)

    pow2 = n_mem & (n_mem - 1) == 0 and rows % n_mem == 0
    blk = rows // max(n_mem // 2, 1)
    start = _block_start("mem", n_mem, rows) if pow2 else 0

    outs = []
    cf_next = col_factor
    for l in range(n_lev):
        a = anom_t[l]
        expanded = expanded_all[l]
        fields = jnp.einsum("mrc,nc->mrn", expanded, cf_next, preferred_element_type=jnp.float32)
        inc = jnp.sum(a.astype(jnp.float32) * fields, axis=0)
        if l == 0:
            precision, inc = lax.optimization_barrier((precision, inc))
            prec_t = jnp.transpose(precision, (1, 0, 2))
        prec = prec_t[l]
        if pow2:
            part, cf_next = _reduce_scatter_rows(inc, "mem", n_mem, jnp.bfloat16, col_factor)
            w_blk = (lax.dynamic_slice_in_dim(prec, start, blk, 0) * part).astype(jnp.bfloat16)
            weighted = _all_gather_rows(w_blk, "mem", n_mem)
        else:
            weighted = (prec * lax.psum(inc, "mem")).astype(jnp.bfloat16)
        scaled = (a.astype(jnp.float32) * weighted.astype(jnp.float32)[None]).astype(jnp.bfloat16)
        projected = jnp.einsum(
            "mrn,nc->mrc", scaled, col_factor, preferred_element_type=jnp.float32
        ).astype(jnp.bfloat16)
        n_m = projected.shape[0]
        cuts = [i * n_m // 3 for i in range(4)]
        chunks = [(lo, hi) for lo, hi in zip(cuts[:-1], cuts[1:]) if lo < hi]
        rf_for_partner = lax.dynamic_slice_in_dim(rf_partner, h * kh, kh, 1)
        summed = jnp.einsum("rk,mrc->kmc", rf_own, projected, preferred_element_type=jnp.float32)
        other = []
        for lo, hi in chunks:
            proj_other = _swap(projected[lo:hi], "half")
            other.append(jnp.einsum(
                "rk,mrc->kmc", rf_for_partner, proj_other, preferred_element_type=jnp.float32
            ))
        summed = summed + jnp.concatenate(other, axis=1)
        outs.append(summed)
    return (control.astype(jnp.float32) + jnp.stack(outs, axis=2)).astype(jnp.bfloat16)


def solution(mesh):
    n_mem = mesh.shape["mem"]

    def f(anomalies, control, precision, row_factor, col_factor):
        return local(anomalies, control, precision, row_factor, col_factor, n_mem)

    return jax.shard_map(
        f,
        mesh=mesh,
        in_specs=(
            P("half", ("grp", "mem"), "lev", None),
            P("half", ("grp", "mem"), "lev", None),
            P("half", ("grp", "lev"), None),
            P("half", None),
            P(),
        ),
        out_specs=P("half", ("grp", "mem"), "lev", None),
        check_vma=False,
    )
```

```python
import jax
import jax.numpy as jnp
from jax import lax
from jax.sharding import PartitionSpec as P


def _swap(x, axis):
    return lax.ppermute(x, axis, [(0, 1), (1, 0)])


def _reduce_scatter_rows(x, axis, size, wire, hold):
    idx = lax.axis_index(axis)
    d = 1
    first = True
    while 2 * d < size:
        half = x.shape[0] // 2
        bit = (idx // d) % 2
        keep = lax.dynamic_slice_in_dim(x, bit * half, half, 0)
        send = lax.dynamic_slice_in_dim(x, (1 - bit) * half, half, 0).astype(wire)
        if first:
            send, hold = lax.optimization_barrier((send, hold))
            first = False
        recv = lax.ppermute(send, axis, [(i, i ^ d) for i in range(size)])
        x = keep + recv.astype(x.dtype)
        d *= 2
    if d < size:
        send = x.astype(wire)
        if first:
            send, hold = lax.optimization_barrier((send, hold))
        recv = lax.ppermute(send, axis, [(i, i ^ d) for i in range(size)])
        x = x + recv.astype(x.dtype)
    return x, hold


def _all_gather_rows(x, axis, size):
    idx = lax.axis_index(axis)
    d = size // 4
    while d >= 1:
        bit = (idx // d) % 2
        recv = lax.ppermute(x, axis, [(i, i ^ d) for i in range(size)])
        lo = jnp.where(bit == 0, x, recv)
        hi = jnp.where(bit == 0, recv, x)
        x = jnp.concatenate([lo, hi], axis=0)
        d //= 2
    return x


def _block_start(axis, size, rows):
    idx = lax.axis_index(axis)
    start = 0
    d, span = 1, rows
    while 2 * d < size:
        span //= 2
        start = start + ((idx // d) % 2) * span
        d *= 2
    return start


def local(anomalies, control, precision, row_factor, col_factor, n_mem):
    h = lax.axis_index("half")
    kh = control.shape[0]
    rows = anomalies.shape[0]
    n_lev = anomalies.shape[2]

    anom_t = jnp.transpose(anomalies, (2, 1, 0, 3))

    rf_own = lax.dynamic_slice_in_dim(row_factor, h * kh, kh, 1)
    rf_other = lax.dynamic_slice_in_dim(row_factor, (1 - h) * kh, kh, 1)
    rf_for_partner = _swap(rf_other, "half")
    ctrl_other = _swap(control, "half")
    expanded_all = (
        jnp.einsum("rk,kmlc->lmrc", rf_own, control, preferred_element_type=jnp.float32)
        + jnp.einsum("rk,kmlc->lmrc", rf_other, ctrl_other, preferred_element_type=jnp.float32)
    ).astype(jnp.bfloat16)

    pow2 = n_mem & (n_mem - 1) == 0 and rows % n_mem == 0
    blk = rows // max(n_mem // 2, 1)
    start = _block_start("mem", n_mem, rows) if pow2 else 0

    outs = []
    cf_next = col_factor
    for l in range(n_lev):
        a = anom_t[l]
        expanded = expanded_all[l]
        fields = jnp.einsum("mrc,nc->mrn", expanded, cf_next, preferred_element_type=jnp.float32)
        inc = jnp.sum(a.astype(jnp.float32) * fields, axis=0)
        if l == 0:
            precision, inc = lax.optimization_barrier((precision, inc))
            prec_t = jnp.transpose(precision, (1, 0, 2))
        prec = prec_t[l]
        if pow2:
            part, cf_next = _reduce_scatter_rows(inc, "mem", n_mem, jnp.bfloat16, col_factor)
            w_blk = (lax.dynamic_slice_in_dim(prec, start, blk, 0) * part).astype(jnp.bfloat16)
            weighted = _all_gather_rows(w_blk, "mem", n_mem)
        else:
            weighted = (prec * lax.psum(inc, "mem")).astype(jnp.bfloat16)
        scaled = (a.astype(jnp.float32) * weighted.astype(jnp.float32)[None]).astype(jnp.bfloat16)
        projected = jnp.einsum(
            "mrn,nc->mrc", scaled, col_factor, preferred_element_type=jnp.float32
        ).astype(jnp.bfloat16)
        n_m = projected.shape[0]
        cuts = [i * n_m // 2 for i in range(3)]
        chunks = [(lo, hi) for lo, hi in zip(cuts[:-1], cuts[1:]) if lo < hi]
        summed = jnp.einsum("rk,mrc->kmc", rf_own, projected, preferred_element_type=jnp.float32)
        other = []
        for lo, hi in chunks:
            proj_other = _swap(projected[lo:hi], "half")
            other.append(jnp.einsum(
                "rk,mrc->kmc", rf_for_partner, proj_other, preferred_element_type=jnp.float32
            ))
        summed = summed + jnp.concatenate(other, axis=1)
        outs.append(summed)
    return (control.astype(jnp.float32) + jnp.stack(outs, axis=2)).astype(jnp.bfloat16)


def solution(mesh):
    n_mem = mesh.shape["mem"]

    def f(anomalies, control, precision, row_factor, col_factor):
        return local(anomalies, control, precision, row_factor, col_factor, n_mem)

    return jax.shard_map(
        f,
        mesh=mesh,
        in_specs=(
            P("half", ("grp", "mem"), "lev", None),
            P("half", ("grp", "mem"), "lev", None),
            P("half", ("grp", "lev"), None),
            P("half", None),
            P(),
        ),
        out_specs=P("half", ("grp", "mem"), "lev", None),
        check_vma=False,
    )
```

```python
import jax
import jax.numpy as jnp
from jax import lax
from jax.sharding import PartitionSpec as P


def _swap(x, axis):
    return lax.ppermute(x, axis, [(0, 1), (1, 0)])


def _reduce_scatter_rows(x, axis, size, wire, hold):
    idx = lax.axis_index(axis)
    d = 1
    first = True
    while 2 * d < size:
        half = x.shape[0] // 2
        bit = (idx // d) % 2
        keep = lax.dynamic_slice_in_dim(x, bit * half, half, 0)
        send = lax.dynamic_slice_in_dim(x, (1 - bit) * half, half, 0).astype(wire)
        if first:
            send, hold = lax.optimization_barrier((send, hold))
            first = False
        recv = lax.ppermute(send, axis, [(i, i ^ d) for i in range(size)])
        x = keep + recv.astype(x.dtype)
        d *= 2
    if d < size:
        send = x.astype(wire)
        if first:
            send, hold = lax.optimization_barrier((send, hold))
        recv = lax.ppermute(send, axis, [(i, i ^ d) for i in range(size)])
        x = x + recv.astype(x.dtype)
    return x, hold


def _all_gather_rows(x, axis, size):
    idx = lax.axis_index(axis)
    d = size // 4
    while d >= 1:
        bit = (idx // d) % 2
        recv = lax.ppermute(x, axis, [(i, i ^ d) for i in range(size)])
        lo = jnp.where(bit == 0, x, recv)
        hi = jnp.where(bit == 0, recv, x)
        x = jnp.concatenate([lo, hi], axis=0)
        d //= 2
    return x


def _block_start(axis, size, rows):
    idx = lax.axis_index(axis)
    start = 0
    d, span = 1, rows
    while 2 * d < size:
        span //= 2
        start = start + ((idx // d) % 2) * span
        d *= 2
    return start


def local(anomalies, control, precision, row_factor, col_factor, n_mem):
    h = lax.axis_index("half")
    kh = control.shape[0]
    rows = anomalies.shape[0]
    n_lev = anomalies.shape[2]

    anom_t = jnp.transpose(anomalies, (2, 1, 0, 3))

    rf_own = lax.dynamic_slice_in_dim(row_factor, h * kh, kh, 1)
    rf_other = lax.dynamic_slice_in_dim(row_factor, (1 - h) * kh, kh, 1)
    rf_for_partner = _swap(rf_other, "half")
    ctrl_other = _swap(control, "half")
    expanded_all = (
        jnp.einsum("rk,kmlc->lmrc", rf_own, control, preferred_element_type=jnp.float32)
        + jnp.einsum("rk,kmlc->lmrc", rf_other, ctrl_other, preferred_element_type=jnp.float32)
    ).astype(jnp.bfloat16)

    pow2 = n_mem & (n_mem - 1) == 0 and rows % n_mem == 0
    blk = rows // max(n_mem // 2, 1)
    start = _block_start("mem", n_mem, rows) if pow2 else 0

    outs = []
    cf_next = col_factor
    for l in range(n_lev):
        a = anom_t[l]
        expanded = expanded_all[l]
        fields = jnp.einsum("mrc,nc->mrn", expanded, cf_next, preferred_element_type=jnp.float32)
        inc = jnp.sum(a.astype(jnp.float32) * fields, axis=0)
        if l == 0:
            precision, inc = lax.optimization_barrier((precision, inc))
            prec_t = jnp.transpose(precision, (1, 0, 2))
        prec = prec_t[l]
        if pow2:
            part, cf_next = _reduce_scatter_rows(inc, "mem", n_mem, jnp.bfloat16, col_factor)
            w_blk = (lax.dynamic_slice_in_dim(prec, start, blk, 0) * part).astype(jnp.bfloat16)
            weighted = _all_gather_rows(w_blk, "mem", n_mem)
        else:
            weighted = (prec * lax.psum(inc, "mem")).astype(jnp.bfloat16)
        scaled = (a.astype(jnp.float32) * weighted.astype(jnp.float32)[None]).astype(jnp.bfloat16)
        projected = jnp.einsum(
            "mrn,nc->mrc", scaled, col_factor, preferred_element_type=jnp.float32
        ).astype(jnp.bfloat16)
        n_m = projected.shape[0]
        cuts = [0, n_m]
        chunks = [(lo, hi) for lo, hi in zip(cuts[:-1], cuts[1:]) if lo < hi]
        summed = jnp.einsum("rk,mrc->kmc", rf_own, projected, preferred_element_type=jnp.float32)
        other = []
        for lo, hi in chunks:
            proj_other = _swap(projected[lo:hi], "half")
            other.append(jnp.einsum(
                "rk,mrc->kmc", rf_for_partner, proj_other, preferred_element_type=jnp.float32
            ))
        summed = summed + jnp.concatenate(other, axis=1)
        outs.append(summed)
    return (control.astype(jnp.float32) + jnp.stack(outs, axis=2)).astype(jnp.bfloat16)


def solution(mesh):
    n_mem = mesh.shape["mem"]

    def f(anomalies, control, precision, row_factor, col_factor):
        return local(anomalies, control, precision, row_factor, col_factor, n_mem)

    return jax.shard_map(
        f,
        mesh=mesh,
        in_specs=(
            P("half", ("grp", "mem"), "lev", None),
            P("half", ("grp", "mem"), "lev", None),
            P("half", ("grp", "lev"), None),
            P("half", None),
            P(),
        ),
        out_specs=P("half", ("grp", "mem"), "lev", None),
        check_vma=False,
    )
```

```python
import jax
import jax.numpy as jnp
from jax import lax
from jax.sharding import PartitionSpec as P


def _swap(x, axis):
    return lax.ppermute(x, axis, [(0, 1), (1, 0)])


def _reduce_scatter_rows(x, axis, size, wire, hold):
    idx = lax.axis_index(axis)
    d = 1
    first = True
    while 2 * d < size:
        half = x.shape[0] // 2
        bit = (idx // d) % 2
        keep = lax.dynamic_slice_in_dim(x, bit * half, half, 0)
        send = lax.dynamic_slice_in_dim(x, (1 - bit) * half, half, 0).astype(wire)
        if first:
            send, hold = lax.optimization_barrier((send, hold))
            first = False
        recv = lax.ppermute(send, axis, [(i, i ^ d) for i in range(size)])
        x = keep + recv.astype(x.dtype)
        d *= 2
    if d < size:
        send = x.astype(wire)
        if first:
            send, hold = lax.optimization_barrier((send, hold))
        recv = lax.ppermute(send, axis, [(i, i ^ d) for i in range(size)])
        x = x + recv.astype(x.dtype)
    return x, hold


def _all_gather_rows(x, axis, size):
    idx = lax.axis_index(axis)
    d = size // 4
    while d >= 1:
        bit = (idx // d) % 2
        recv = lax.ppermute(x, axis, [(i, i ^ d) for i in range(size)])
        lo = jnp.where(bit == 0, x, recv)
        hi = jnp.where(bit == 0, recv, x)
        x = jnp.concatenate([lo, hi], axis=0)
        d //= 2
    return x


def _block_start(axis, size, rows):
    idx = lax.axis_index(axis)
    start = 0
    d, span = 1, rows
    while 2 * d < size:
        span //= 2
        start = start + ((idx // d) % 2) * span
        d *= 2
    return start


def local(anomalies, control, precision, row_factor, col_factor, n_mem):
    h = lax.axis_index("half")
    kh = control.shape[0]
    rows = anomalies.shape[0]
    n_lev = anomalies.shape[2]

    anom_t = jnp.transpose(anomalies, (2, 1, 0, 3))

    rf_own = lax.dynamic_slice_in_dim(row_factor, h * kh, kh, 1)
    rf_other = lax.dynamic_slice_in_dim(row_factor, (1 - h) * kh, kh, 1)
    ctrl_other = _swap(control, "half")
    expanded_all = (
        jnp.einsum("rk,kmlc->lmrc", rf_own, control, preferred_element_type=jnp.float32)
        + jnp.einsum("rk,kmlc->lmrc", rf_other, ctrl_other, preferred_element_type=jnp.float32)
    ).astype(jnp.bfloat16)

    pow2 = n_mem & (n_mem - 1) == 0 and rows % n_mem == 0
    blk = rows // max(n_mem // 2, 1)
    start = _block_start("mem", n_mem, rows) if pow2 else 0

    outs = []
    cf_next = col_factor
    for l in range(n_lev):
        a = anom_t[l]
        expanded = expanded_all[l]
        fields = jnp.einsum("mrc,nc->mrn", expanded, cf_next, preferred_element_type=jnp.float32)
        inc = jnp.sum(a.astype(jnp.float32) * fields, axis=0)
        if l == 0:
            precision, inc = lax.optimization_barrier((precision, inc))
            prec_t = jnp.transpose(precision, (1, 0, 2))
        prec = prec_t[l]
        if pow2:
            part, cf_next = _reduce_scatter_rows(inc, "mem", n_mem, jnp.bfloat16, col_factor)
            w_blk = (lax.dynamic_slice_in_dim(prec, start, blk, 0) * part).astype(jnp.bfloat16)
            weighted = _all_gather_rows(w_blk, "mem", n_mem)
        else:
            weighted = (prec * lax.psum(inc, "mem")).astype(jnp.bfloat16)
        scaled = (a.astype(jnp.float32) * weighted.astype(jnp.float32)[None]).astype(jnp.bfloat16)
        projected = jnp.einsum(
            "mrn,nc->mrc", scaled, col_factor, preferred_element_type=jnp.float32
        ).astype(jnp.bfloat16)
        n_m = projected.shape[0]
        cuts = [0, n_m]
        chunks = [(lo, hi) for lo, hi in zip(cuts[:-1], cuts[1:]) if lo < hi]
        summed = jnp.einsum("rk,mrc->kmc", rf_own, projected, preferred_element_type=jnp.float32)
        other = []
        for lo, hi in chunks:
            for_partner = jnp.einsum(
                "rk,mrc->kmc", rf_other, projected[lo:hi], preferred_element_type=jnp.float32
            )
            other.append(_swap(for_partner, "half"))
        summed = summed + jnp.concatenate(other, axis=1)
        outs.append(summed)
    return (control.astype(jnp.float32) + jnp.stack(outs, axis=2)).astype(jnp.bfloat16)


def solution(mesh):
    n_mem = mesh.shape["mem"]

    def f(anomalies, control, precision, row_factor, col_factor):
        return local(anomalies, control, precision, row_factor, col_factor, n_mem)

    return jax.shard_map(
        f,
        mesh=mesh,
        in_specs=(
            P("half", ("grp", "mem"), "lev", None),
            P("half", ("grp", "mem"), "lev", None),
            P("half", ("grp", "lev"), None),
            P("half", None),
            P(),
        ),
        out_specs=P("half", ("grp", "mem"), "lev", None),
        check_vma=False,
    )
```

```python
import jax
import jax.numpy as jnp
from jax import lax
from jax.sharding import PartitionSpec as P


def _swap(x, axis):
    return lax.ppermute(x, axis, [(0, 1), (1, 0)])


def _reduce_scatter_rows(x, axis, size, wire, hold):
    idx = lax.axis_index(axis)
    d = 1
    first = True
    while 2 * d < size:
        half = x.shape[0] // 2
        bit = (idx // d) % 2
        keep = lax.dynamic_slice_in_dim(x, bit * half, half, 0)
        send = lax.dynamic_slice_in_dim(x, (1 - bit) * half, half, 0).astype(wire)
        if first:
            send, hold = lax.optimization_barrier((send, hold))
            first = False
        recv = lax.ppermute(send, axis, [(i, i ^ d) for i in range(size)])
        x = keep + recv.astype(x.dtype)
        d *= 2
    if d < size:
        send = x.astype(wire)
        if first:
            send, hold = lax.optimization_barrier((send, hold))
        recv = lax.ppermute(send, axis, [(i, i ^ d) for i in range(size)])
        x = x + recv.astype(x.dtype)
    return x, hold


def _all_gather_rows(x, axis, size):
    idx = lax.axis_index(axis)
    d = size // 4
    while d >= 1:
        bit = (idx // d) % 2
        recv = lax.ppermute(x, axis, [(i, i ^ d) for i in range(size)])
        lo = jnp.where(bit == 0, x, recv)
        hi = jnp.where(bit == 0, recv, x)
        x = jnp.concatenate([lo, hi], axis=0)
        d //= 2
    return x


def _block_start(axis, size, rows):
    idx = lax.axis_index(axis)
    start = 0
    d, span = 1, rows
    while 2 * d < size:
        span //= 2
        start = start + ((idx // d) % 2) * span
        d *= 2
    return start


def local(anomalies, control, precision, row_factor, col_factor, n_mem):
    h = lax.axis_index("half")
    kh = control.shape[0]
    rows = anomalies.shape[0]
    n_lev = anomalies.shape[2]

    anom_t = jnp.transpose(anomalies, (2, 1, 0, 3))

    rf_own = lax.dynamic_slice_in_dim(row_factor, h * kh, kh, 1)
    rf_other = lax.dynamic_slice_in_dim(row_factor, (1 - h) * kh, kh, 1)
    ctrl_other = _swap(control, "half")
    expanded_all = (
        jnp.einsum("rk,kmlc->lmrc", rf_own, control, preferred_element_type=jnp.float32)
        + jnp.einsum("rk,kmlc->lmrc", rf_other, ctrl_other, preferred_element_type=jnp.float32)
    ).astype(jnp.bfloat16)

    pow2 = n_mem & (n_mem - 1) == 0 and rows % n_mem == 0
    blk = rows // max(n_mem // 2, 1)
    start = _block_start("mem", n_mem, rows) if pow2 else 0

    outs = []
    cf_next = col_factor
    for l in range(n_lev):
        a = anom_t[l]
        expanded = expanded_all[l]
        fields = jnp.einsum("mrc,nc->mrn", expanded, cf_next, preferred_element_type=jnp.float32)
        inc = jnp.sum(a.astype(jnp.float32) * fields, axis=0)
        if l == 0:
            precision, inc = lax.optimization_barrier((precision, inc))
            prec_t = jnp.transpose(precision, (1, 0, 2))
        prec = prec_t[l]
        if pow2:
            part, cf_next = _reduce_scatter_rows(inc, "mem", n_mem, jnp.bfloat16, col_factor)
            w_blk = (lax.dynamic_slice_in_dim(prec, start, blk, 0) * part).astype(jnp.bfloat16)
            weighted = _all_gather_rows(w_blk, "mem", n_mem)
        else:
            weighted = (prec * lax.psum(inc, "mem")).astype(jnp.bfloat16)
        scaled = (a.astype(jnp.float32) * weighted.astype(jnp.float32)[None]).astype(jnp.bfloat16)
        projected = jnp.einsum(
            "mrn,nc->mrc", scaled, col_factor, preferred_element_type=jnp.float32
        ).astype(jnp.bfloat16)
        n_m = projected.shape[0]
        cuts = [0, n_m]
        chunks = [(lo, hi) for lo, hi in zip(cuts[:-1], cuts[1:]) if lo < hi]
        summed = jnp.einsum("rk,mrc->kmc", rf_own, projected, preferred_element_type=jnp.float32)
        other = []
        for lo, hi in chunks:
            for_partner = jnp.einsum(
                "rk,mrc->kmc", rf_other, projected[lo:hi], preferred_element_type=jnp.float32
            )
            other.append(_swap(for_partner.astype(jnp.bfloat16), "half").astype(jnp.float32))
        summed = summed + jnp.concatenate(other, axis=1)
        outs.append(summed)
    return (control.astype(jnp.float32) + jnp.stack(outs, axis=2)).astype(jnp.bfloat16)


def solution(mesh):
    n_mem = mesh.shape["mem"]

    def f(anomalies, control, precision, row_factor, col_factor):
        return local(anomalies, control, precision, row_factor, col_factor, n_mem)

    return jax.shard_map(
        f,
        mesh=mesh,
        in_specs=(
            P("half", ("grp", "mem"), "lev", None),
            P("half", ("grp", "mem"), "lev", None),
            P("half", ("grp", "lev"), None),
            P("half", None),
            P(),
        ),
        out_specs=P("half", ("grp", "mem"), "lev", None),
        check_vma=False,
    )
```

```python
import jax
import jax.numpy as jnp
from jax import lax
from jax.sharding import PartitionSpec as P


def _swap(x, axis):
    return lax.ppermute(x, axis, [(0, 1), (1, 0)])


def _reduce_scatter_rows(x, axis, size, wire, hold):
    idx = lax.axis_index(axis)
    d = 1
    first = True
    while 2 * d < size:
        half = x.shape[0] // 2
        bit = (idx // d) % 2
        keep = lax.dynamic_slice_in_dim(x, bit * half, half, 0)
        send = lax.dynamic_slice_in_dim(x, (1 - bit) * half, half, 0).astype(wire)
        if first:
            send, hold = lax.optimization_barrier((send, hold))
            first = False
        recv = lax.ppermute(send, axis, [(i, i ^ d) for i in range(size)])
        x = keep + recv.astype(x.dtype)
        d *= 2
    if d < size:
        send = x.astype(wire)
        if first:
            send, hold = lax.optimization_barrier((send, hold))
        recv = lax.ppermute(send, axis, [(i, i ^ d) for i in range(size)])
        x = x + recv.astype(x.dtype)
    return x, hold


def _all_gather_rows(x, axis, size):
    idx = lax.axis_index(axis)
    d = size // 4
    while d >= 1:
        bit = (idx // d) % 2
        recv = lax.ppermute(x, axis, [(i, i ^ d) for i in range(size)])
        lo = jnp.where(bit == 0, x, recv)
        hi = jnp.where(bit == 0, recv, x)
        x = jnp.concatenate([lo, hi], axis=0)
        d //= 2
    return x


def _block_start(axis, size, rows):
    idx = lax.axis_index(axis)
    start = 0
    d, span = 1, rows
    while 2 * d < size:
        span //= 2
        start = start + ((idx // d) % 2) * span
        d *= 2
    return start


def local(anomalies, control, precision, row_factor, col_factor, n_mem):
    h = lax.axis_index("half")
    kh = control.shape[0]
    rows = anomalies.shape[0]
    n_lev = anomalies.shape[2]

    anom_t = jnp.transpose(anomalies, (2, 1, 0, 3))

    rf_own = lax.dynamic_slice_in_dim(row_factor, h * kh, kh, 1)
    rf_other = lax.dynamic_slice_in_dim(row_factor, (1 - h) * kh, kh, 1)
    ctrl_other = _swap(control, "half")
    expanded_all = (
        jnp.einsum("rk,kmlc->lmrc", rf_own, control, preferred_element_type=jnp.float32)
        + jnp.einsum("rk,kmlc->lmrc", rf_other, ctrl_other, preferred_element_type=jnp.float32)
    ).astype(jnp.bfloat16)

    pow2 = n_mem & (n_mem - 1) == 0 and rows % n_mem == 0
    blk = rows // max(n_mem // 2, 1)
    start = _block_start("mem", n_mem, rows) if pow2 else 0

    outs = []
    cf_next = col_factor
    for l in range(n_lev):
        a = anom_t[l]
        expanded = expanded_all[l]
        fields = jnp.einsum("mrc,nc->mrn", expanded, cf_next, preferred_element_type=jnp.float32)
        inc = jnp.sum(a.astype(jnp.float32) * fields, axis=0)
        if l == 0:
            precision, inc = lax.optimization_barrier((precision, inc))
            prec_t = jnp.transpose(precision, (1, 0, 2))
        prec = prec_t[l]
        if pow2:
            part, cf_next = _reduce_scatter_rows(inc, "mem", n_mem, jnp.bfloat16, col_factor)
            w_blk = (lax.dynamic_slice_in_dim(prec, start, blk, 0) * part).astype(jnp.bfloat16)
            weighted = _all_gather_rows(w_blk, "mem", n_mem)
        else:
            weighted = (prec * lax.psum(inc, "mem")).astype(jnp.bfloat16)
        scaled = (a.astype(jnp.float32) * weighted.astype(jnp.float32)[None]).astype(jnp.bfloat16)
        projected = jnp.einsum(
            "mrn,nc->mrc", scaled, col_factor, preferred_element_type=jnp.float32
        ).astype(jnp.bfloat16)
        n_m = projected.shape[0]
        cuts = [0, n_m]
        chunks = [(lo, hi) for lo, hi in zip(cuts[:-1], cuts[1:]) if lo < hi]
        summed = lax.optimization_barrier(
            jnp.einsum("rk,mrc->kmc", rf_own, projected, preferred_element_type=jnp.float32))
        other = []
        for lo, hi in chunks:
            for_partner = jnp.einsum(
                "rk,mrc->kmc", rf_other, projected[lo:hi], preferred_element_type=jnp.float32
            )
            other.append(_swap(for_partner, "half"))
        summed = summed + jnp.concatenate(other, axis=1)
        outs.append(summed)
    return (control.astype(jnp.float32) + jnp.stack(outs, axis=2)).astype(jnp.bfloat16)


def solution(mesh):
    n_mem = mesh.shape["mem"]

    def f(anomalies, control, precision, row_factor, col_factor):
        return local(anomalies, control, precision, row_factor, col_factor, n_mem)

    return jax.shard_map(
        f,
        mesh=mesh,
        in_specs=(
            P("half", ("grp", "mem"), "lev", None),
            P("half", ("grp", "mem"), "lev", None),
            P("half", ("grp", "lev"), None),
            P("half", None),
            P(),
        ),
        out_specs=P("half", ("grp", "mem"), "lev", None),
        check_vma=False,
    )
```

```python
import jax
import jax.numpy as jnp
from jax import lax
from jax.sharding import PartitionSpec as P


def _swap(x, axis):
    return lax.ppermute(x, axis, [(0, 1), (1, 0)])


def _reduce_scatter_rows(x, axis, size, wire, hold):
    idx = lax.axis_index(axis)
    d = 1
    first = True
    while 2 * d < size:
        half = x.shape[0] // 2
        bit = (idx // d) % 2
        keep = lax.dynamic_slice_in_dim(x, bit * half, half, 0)
        send = lax.dynamic_slice_in_dim(x, (1 - bit) * half, half, 0).astype(wire)
        if first:
            send, hold = lax.optimization_barrier((send, hold))
            first = False
        recv = lax.ppermute(send, axis, [(i, i ^ d) for i in range(size)])
        x = keep + recv.astype(x.dtype)
        d *= 2
    if d < size:
        send = x.astype(wire)
        if first:
            send, hold = lax.optimization_barrier((send, hold))
        recv = lax.ppermute(send, axis, [(i, i ^ d) for i in range(size)])
        x = x + recv.astype(x.dtype)
    return x, hold


def _all_gather_rows(x, axis, size):
    idx = lax.axis_index(axis)
    d = size // 4
    while d >= 1:
        bit = (idx // d) % 2
        recv = lax.ppermute(x, axis, [(i, i ^ d) for i in range(size)])
        lo = jnp.where(bit == 0, x, recv)
        hi = jnp.where(bit == 0, recv, x)
        x = jnp.concatenate([lo, hi], axis=0)
        d //= 2
    return x


def _block_start(axis, size, rows):
    idx = lax.axis_index(axis)
    start = 0
    d, span = 1, rows
    while 2 * d < size:
        span //= 2
        start = start + ((idx // d) % 2) * span
        d *= 2
    return start


def local(anomalies, control, precision, row_factor, col_factor, n_mem):
    h = lax.axis_index("half")
    kh = control.shape[0]
    rows = anomalies.shape[0]
    n_lev = anomalies.shape[2]

    anom_t = jnp.transpose(anomalies, (2, 1, 0, 3))

    rf_own = lax.dynamic_slice_in_dim(row_factor, h * kh, kh, 1)
    rf_other = lax.dynamic_slice_in_dim(row_factor, (1 - h) * kh, kh, 1)
    ctrl_other = _swap(control, "half")
    ctrl_full = jnp.where(
        h == 0,
        jnp.concatenate([control, ctrl_other], axis=0),
        jnp.concatenate([ctrl_other, control], axis=0),
    )
    expanded_all = jnp.einsum(
        "rk,kmlc->lmrc", row_factor, ctrl_full, preferred_element_type=jnp.float32
    ).astype(jnp.bfloat16)

    pow2 = n_mem & (n_mem - 1) == 0 and rows % n_mem == 0
    blk = rows // max(n_mem // 2, 1)
    start = _block_start("mem", n_mem, rows) if pow2 else 0

    outs = []
    cf_next = col_factor
    for l in range(n_lev):
        a = anom_t[l]
        expanded = expanded_all[l]
        fields = jnp.einsum("mrc,nc->mrn", expanded, cf_next, preferred_element_type=jnp.float32)
        inc = jnp.sum(a.astype(jnp.float32) * fields, axis=0)
        if l == 0:
            precision, inc = lax.optimization_barrier((precision, inc))
            prec_t = jnp.transpose(precision, (1, 0, 2))
        prec = prec_t[l]
        if pow2:
            part, cf_next = _reduce_scatter_rows(inc, "mem", n_mem, jnp.bfloat16, col_factor)
            w_blk = (lax.dynamic_slice_in_dim(prec, start, blk, 0) * part).astype(jnp.bfloat16)
            weighted = _all_gather_rows(w_blk, "mem", n_mem)
        else:
            weighted = (prec * lax.psum(inc, "mem")).astype(jnp.bfloat16)
        scaled = (a.astype(jnp.float32) * weighted.astype(jnp.float32)[None]).astype(jnp.bfloat16)
        projected = jnp.einsum(
            "mrn,nc->mrc", scaled, col_factor, preferred_element_type=jnp.float32
        ).astype(jnp.bfloat16)
        n_m = projected.shape[0]
        cuts = [0, n_m]
        chunks = [(lo, hi) for lo, hi in zip(cuts[:-1], cuts[1:]) if lo < hi]
        summed = jnp.einsum("rk,mrc->kmc", rf_own, projected, preferred_element_type=jnp.float32)
        other = []
        for lo, hi in chunks:
            for_partner = jnp.einsum(
                "rk,mrc->kmc", rf_other, projected[lo:hi], preferred_element_type=jnp.float32
            )
            other.append(_swap(for_partner, "half"))
        summed = summed + jnp.concatenate(other, axis=1)
        outs.append(summed)
    return (control.astype(jnp.float32) + jnp.stack(outs, axis=2)).astype(jnp.bfloat16)


def solution(mesh):
    n_mem = mesh.shape["mem"]

    def f(anomalies, control, precision, row_factor, col_factor):
        return local(anomalies, control, precision, row_factor, col_factor, n_mem)

    return jax.shard_map(
        f,
        mesh=mesh,
        in_specs=(
            P("half", ("grp", "mem"), "lev", None),
            P("half", ("grp", "mem"), "lev", None),
            P("half", ("grp", "lev"), None),
            P("half", None),
            P(),
        ),
        out_specs=P("half", ("grp", "mem"), "lev", None),
        check_vma=False,
    )
```

```python
import jax
import jax.numpy as jnp
from jax import lax
from jax.sharding import PartitionSpec as P


def _swap(x, axis):
    return lax.ppermute(x, axis, [(0, 1), (1, 0)])


def _reduce_scatter_rows(x, axis, size, wire, hold):
    idx = lax.axis_index(axis)
    d = 1
    first = True
    while 2 * d < size:
        half = x.shape[0] // 2
        bit = (idx // d) % 2
        keep = lax.dynamic_slice_in_dim(x, bit * half, half, 0)
        send = lax.dynamic_slice_in_dim(x, (1 - bit) * half, half, 0).astype(wire)
        if first:
            send, hold = lax.optimization_barrier((send, hold))
            first = False
        recv = lax.ppermute(send, axis, [(i, i ^ d) for i in range(size)])
        x = keep + recv.astype(x.dtype)
        d *= 2
    if d < size:
        send = x.astype(wire)
        if first:
            send, hold = lax.optimization_barrier((send, hold))
        recv = lax.ppermute(send, axis, [(i, i ^ d) for i in range(size)])
        x = x + recv.astype(x.dtype)
    return x, hold


def _all_gather_rows(x, axis, size):
    idx = lax.axis_index(axis)
    d = size // 4
    while d >= 1:
        bit = (idx // d) % 2
        recv = lax.ppermute(x, axis, [(i, i ^ d) for i in range(size)])
        lo = jnp.where(bit == 0, x, recv)
        hi = jnp.where(bit == 0, recv, x)
        x = jnp.concatenate([lo, hi], axis=0)
        d //= 2
    return x


def _block_start(axis, size, rows):
    idx = lax.axis_index(axis)
    start = 0
    d, span = 1, rows
    while 2 * d < size:
        span //= 2
        start = start + ((idx // d) % 2) * span
        d *= 2
    return start


def local(anomalies, control, precision, row_factor, col_factor, n_mem):
    h = lax.axis_index("half")
    kh = control.shape[0]
    rows = anomalies.shape[0]
    n_lev = anomalies.shape[2]

    anom_t = jnp.transpose(anomalies, (2, 1, 0, 3))

    rf_own = lax.dynamic_slice_in_dim(row_factor, h * kh, kh, 1)
    rf_other = lax.dynamic_slice_in_dim(row_factor, (1 - h) * kh, kh, 1)
    ctrl_other = _swap(control, "half")
    expanded_all = (
        jnp.einsum("rk,kmlc->lmrc", rf_own, control, preferred_element_type=jnp.float32)
        + jnp.einsum("rk,kmlc->lmrc", rf_other, ctrl_other, preferred_element_type=jnp.float32)
    ).astype(jnp.bfloat16)

    pow2 = n_mem & (n_mem - 1) == 0 and rows % n_mem == 0
    blk = rows // max(n_mem // 2, 1)
    start = _block_start("mem", n_mem, rows) if pow2 else 0

    outs = []
    cf_next = col_factor
    parts = []
    for l in range(n_lev):
        a = anom_t[l]
        expanded = expanded_all[l]
        fields = jnp.einsum("mrc,nc->mrn", expanded, cf_next, preferred_element_type=jnp.float32)
        inc = jnp.sum(a.astype(jnp.float32) * fields, axis=0)
        if pow2:
            if l + 1 < n_lev:
                part, cf_next = _reduce_scatter_rows(inc, "mem", n_mem, jnp.bfloat16, col_factor)
            else:
                part, precision = _reduce_scatter_rows(inc, "mem", n_mem, jnp.bfloat16, precision)
        else:
            part = inc
        parts.append(part)
    prec_t = jnp.transpose(precision, (1, 0, 2))
    for l in range(n_lev):
        a = anom_t[l]
        part = parts[l]
        prec = prec_t[l]
        if pow2:
            w_blk = (lax.dynamic_slice_in_dim(prec, start, blk, 0) * part).astype(jnp.bfloat16)
            weighted = _all_gather_rows(w_blk, "mem", n_mem)
        else:
            weighted = (prec * lax.psum(part, "mem")).astype(jnp.bfloat16)
        scaled = (a.astype(jnp.float32) * weighted.astype(jnp.float32)[None]).astype(jnp.bfloat16)
        projected = jnp.einsum(
            "mrn,nc->mrc", scaled, col_factor, preferred_element_type=jnp.float32
        ).astype(jnp.bfloat16)
        n_m = projected.shape[0]
        cuts = [0, n_m]
        chunks = [(lo, hi) for lo, hi in zip(cuts[:-1], cuts[1:]) if lo < hi]
        summed = jnp.einsum("rk,mrc->kmc", rf_own, projected, preferred_element_type=jnp.float32)
        other = []
        for lo, hi in chunks:
            for_partner = jnp.einsum(
                "rk,mrc->kmc", rf_other, projected[lo:hi], preferred_element_type=jnp.float32
            )
            other.append(_swap(for_partner, "half"))
        summed = summed + jnp.concatenate(other, axis=1)
        outs.append(summed)
    return (control.astype(jnp.float32) + jnp.stack(outs, axis=2)).astype(jnp.bfloat16)


def solution(mesh):
    n_mem = mesh.shape["mem"]

    def f(anomalies, control, precision, row_factor, col_factor):
        return local(anomalies, control, precision, row_factor, col_factor, n_mem)

    return jax.shard_map(
        f,
        mesh=mesh,
        in_specs=(
            P("half", ("grp", "mem"), "lev", None),
            P("half", ("grp", "mem"), "lev", None),
            P("half", ("grp", "lev"), None),
            P("half", None),
            P(),
        ),
        out_specs=P("half", ("grp", "mem"), "lev", None),
        check_vma=False,
    )
```

```python
import jax
import jax.numpy as jnp
from jax import lax
from jax.sharding import PartitionSpec as P


def _swap(x, axis):
    return lax.ppermute(x, axis, [(0, 1), (1, 0)])


def _reduce_scatter_rows(x, axis, size, wire, hold):
    idx = lax.axis_index(axis)
    d = 1
    first = True
    while 2 * d < size:
        half = x.shape[0] // 2
        bit = (idx // d) % 2
        keep = lax.dynamic_slice_in_dim(x, bit * half, half, 0)
        send = lax.dynamic_slice_in_dim(x, (1 - bit) * half, half, 0).astype(wire)
        if first:
            send, hold = lax.optimization_barrier((send, hold))
            first = False
        recv = lax.ppermute(send, axis, [(i, i ^ d) for i in range(size)])
        x = keep + recv.astype(x.dtype)
        d *= 2
    if d < size:
        send = x.astype(wire)
        if first:
            send, hold = lax.optimization_barrier((send, hold))
        recv = lax.ppermute(send, axis, [(i, i ^ d) for i in range(size)])
        x = x + recv.astype(x.dtype)
    return x, hold


def _all_gather_rows(x, axis, size):
    idx = lax.axis_index(axis)
    d = size // 4
    while d >= 1:
        bit = (idx // d) % 2
        recv = lax.ppermute(x, axis, [(i, i ^ d) for i in range(size)])
        lo = jnp.where(bit == 0, x, recv)
        hi = jnp.where(bit == 0, recv, x)
        x = jnp.concatenate([lo, hi], axis=0)
        d //= 2
    return x


def _block_start(axis, size, rows):
    idx = lax.axis_index(axis)
    start = 0
    d, span = 1, rows
    while 2 * d < size:
        span //= 2
        start = start + ((idx // d) % 2) * span
        d *= 2
    return start


def local(anomalies, control, precision, row_factor, col_factor, n_mem):
    h = lax.axis_index("half")
    kh = control.shape[0]
    rows = anomalies.shape[0]
    n_lev = anomalies.shape[2]

    anom_t = jnp.transpose(anomalies, (2, 1, 0, 3))

    rf_own = lax.dynamic_slice_in_dim(row_factor, h * kh, kh, 1)
    rf_other = lax.dynamic_slice_in_dim(row_factor, (1 - h) * kh, kh, 1)
    ctrl_other = _swap(control, "half")
    expanded_all = (
        jnp.einsum("rk,kmlc->lmrc", rf_own, control, preferred_element_type=jnp.float32)
        + jnp.einsum("rk,kmlc->lmrc", rf_other, ctrl_other, preferred_element_type=jnp.float32)
    ).astype(jnp.bfloat16)

    pow2 = n_mem & (n_mem - 1) == 0 and rows % n_mem == 0
    blk = rows // max(n_mem // 2, 1)
    start = _block_start("mem", n_mem, rows) if pow2 else 0

    outs = []
    cf_next = col_factor
    for l in range(n_lev):
        a = anom_t[l]
        expanded = expanded_all[l]
        fields = jnp.einsum("mrc,nc->mrn", expanded, cf_next, preferred_element_type=jnp.float32)
        inc = jnp.sum(a.astype(jnp.float32) * fields, axis=0)
        if l == 0:
            precision, inc = lax.optimization_barrier((precision, inc))
            prec_t = jnp.transpose(precision, (1, 0, 2))
        prec = prec_t[l]
        if pow2:
            part, cf_next = _reduce_scatter_rows(inc, "mem", n_mem, jnp.bfloat16, col_factor)
            w_blk = (lax.dynamic_slice_in_dim(prec, start, blk, 0) * part).astype(jnp.bfloat16)
            weighted = _all_gather_rows(w_blk, "mem", n_mem)
        else:
            weighted = (prec * lax.psum(inc, "mem")).astype(jnp.bfloat16)
        scaled = (a.astype(jnp.float32) * weighted.astype(jnp.float32)[None]).astype(jnp.bfloat16)
        projected = jnp.einsum(
            "mrn,nc->mrc", scaled, col_factor, preferred_element_type=jnp.float32
        ).astype(jnp.bfloat16)
        n_m = projected.shape[0]
        cuts = [i * n_m // 2 for i in range(3)]
        chunks = [(lo, hi) for lo, hi in zip(cuts[:-1], cuts[1:]) if lo < hi]
        summed = jnp.einsum("rk,mrc->kmc", rf_own, projected, preferred_element_type=jnp.float32)
        other = []
        for lo, hi in chunks:
            for_partner = jnp.einsum(
                "rk,mrc->kmc", rf_other, projected[lo:hi], preferred_element_type=jnp.float32
            )
            other.append(_swap(for_partner, "half"))
        summed = summed + jnp.concatenate(other, axis=1)
        outs.append(summed)
    return (control.astype(jnp.float32) + jnp.stack(outs, axis=2)).astype(jnp.bfloat16)


def solution(mesh):
    n_mem = mesh.shape["mem"]

    def f(anomalies, control, precision, row_factor, col_factor):
        return local(anomalies, control, precision, row_factor, col_factor, n_mem)

    return jax.shard_map(
        f,
        mesh=mesh,
        in_specs=(
            P("half", ("grp", "mem"), "lev", None),
            P("half", ("grp", "mem"), "lev", None),
            P("half", ("grp", "lev"), None),
            P("half", None),
            P(),
        ),
        out_specs=P("half", ("grp", "mem"), "lev", None),
        check_vma=False,
    )
```

```python
import jax
import jax.numpy as jnp
from jax import lax
from jax.sharding import PartitionSpec as P


def _swap(x, axis):
    return lax.ppermute(x, axis, [(0, 1), (1, 0)])


def _reduce_scatter_rows(x, axis, size, wire, hold):
    idx = lax.axis_index(axis)
    d = 1
    first = True
    while 2 * d < size:
        half = x.shape[0] // 2
        bit = (idx // d) % 2
        keep = lax.dynamic_slice_in_dim(x, bit * half, half, 0)
        send = lax.dynamic_slice_in_dim(x, (1 - bit) * half, half, 0).astype(wire)
        if first:
            send, hold = lax.optimization_barrier((send, hold))
            first = False
        recv = lax.ppermute(send, axis, [(i, i ^ d) for i in range(size)])
        x = keep + recv.astype(x.dtype)
        d *= 2
    if d < size:
        send = x.astype(wire)
        if first:
            send, hold = lax.optimization_barrier((send, hold))
        recv = lax.ppermute(send, axis, [(i, i ^ d) for i in range(size)])
        x = x + recv.astype(x.dtype)
    return x, hold


def _all_gather_rows(x, axis, size):
    idx = lax.axis_index(axis)
    d = size // 4
    while d >= 1:
        bit = (idx // d) % 2
        recv = lax.ppermute(x, axis, [(i, i ^ d) for i in range(size)])
        lo = jnp.where(bit == 0, x, recv)
        hi = jnp.where(bit == 0, recv, x)
        x = jnp.concatenate([lo, hi], axis=0)
        d //= 2
    return x


def _block_start(axis, size, rows):
    idx = lax.axis_index(axis)
    start = 0
    d, span = 1, rows
    while 2 * d < size:
        span //= 2
        start = start + ((idx // d) % 2) * span
        d *= 2
    return start


def local(anomalies, control, precision, row_factor, col_factor, n_mem):
    h = lax.axis_index("half")
    kh = control.shape[0]
    rows = anomalies.shape[0]
    n_lev = anomalies.shape[2]

    anom_t = jnp.transpose(anomalies, (2, 1, 0, 3))

    rf_own = lax.dynamic_slice_in_dim(row_factor, h * kh, kh, 1)
    rf_other = lax.dynamic_slice_in_dim(row_factor, (1 - h) * kh, kh, 1)
    ctrl_other = _swap(control, "half")
    expanded_all = (
        jnp.einsum("rk,kmlc->lmrc", rf_own, control, preferred_element_type=jnp.float32)
        + jnp.einsum("rk,kmlc->lmrc", rf_other, ctrl_other, preferred_element_type=jnp.float32)
    ).astype(jnp.bfloat16)

    pow2 = n_mem & (n_mem - 1) == 0 and rows % n_mem == 0
    blk = rows // max(n_mem // 2, 1)
    start = _block_start("mem", n_mem, rows) if pow2 else 0

    outs = []
    cf_next = col_factor
    for l in range(n_lev):
        a = anom_t[l]
        expanded = expanded_all[l]
        fields = jnp.einsum("mrc,nc->mrn", expanded, cf_next, preferred_element_type=jnp.float32)
        inc = jnp.sum(a.astype(jnp.float32) * fields, axis=0)
        if l == 0:
            prec_t = jnp.transpose(precision, (1, 0, 2))
        prec = prec_t[l]
        if pow2:
            part, cf_next = _reduce_scatter_rows(inc, "mem", n_mem, jnp.bfloat16, col_factor)
            w_blk = (lax.dynamic_slice_in_dim(prec, start, blk, 0) * part).astype(jnp.bfloat16)
            weighted = _all_gather_rows(w_blk, "mem", n_mem)
        else:
            weighted = (prec * lax.psum(inc, "mem")).astype(jnp.bfloat16)
        scaled = (a.astype(jnp.float32) * weighted.astype(jnp.float32)[None]).astype(jnp.bfloat16)
        projected = jnp.einsum(
            "mrn,nc->mrc", scaled, col_factor, preferred_element_type=jnp.float32
        ).astype(jnp.bfloat16)
        n_m = projected.shape[0]
        cuts = [0, n_m]
        chunks = [(lo, hi) for lo, hi in zip(cuts[:-1], cuts[1:]) if lo < hi]
        summed = jnp.einsum("rk,mrc->kmc", rf_own, projected, preferred_element_type=jnp.float32)
        other = []
        for lo, hi in chunks:
            for_partner = jnp.einsum(
                "rk,mrc->kmc", rf_other, projected[lo:hi], preferred_element_type=jnp.float32
            )
            other.append(_swap(for_partner, "half"))
        summed = summed + jnp.concatenate(other, axis=1)
        outs.append(summed)
    return (control.astype(jnp.float32) + jnp.stack(outs, axis=2)).astype(jnp.bfloat16)


def solution(mesh):
    n_mem = mesh.shape["mem"]

    def f(anomalies, control, precision, row_factor, col_factor):
        return local(anomalies, control, precision, row_factor, col_factor, n_mem)

    return jax.shard_map(
        f,
        mesh=mesh,
        in_specs=(
            P("half", ("grp", "mem"), "lev", None),
            P("half", ("grp", "mem"), "lev", None),
            P("half", ("grp", "lev"), None),
            P("half", None),
            P(),
        ),
        out_specs=P("half", ("grp", "mem"), "lev", None),
        check_vma=False,
    )
```
